32 devices in a mesh: shots: 4 (over x, core), depth: 8 (over z, y).
Axes of the slice: x: 2, y: 2, z: 4, core: 2. Of those that a mesh axis runs over, the one named last changes fastest.
Arguments:
- forward_prev: float32 [4, 64, 128, 256], P('shots', 'depth'), may hold values from -3 to 3
- forward_now: float32 [4, 64, 128, 256], P('shots', 'depth'), may hold values from -3 to 3
- adjoint_prev: float32 [4, 64, 128, 256], P('shots', 'depth'), may hold values from -3 to 3
- adjoint_now: float32 [4, 64, 128, 256], P('shots', 'depth'), may hold values from -3 to 3
- courant: float32 [64, 128, 256], P('depth'), may hold values from 0.05 to 0.18
- wavelet: float32 [2, 512], replicated, may hold values from -5 to 5
- sign_bits: int32 [4, 512], P('shots'), may hold values from 0 to 1
- source_depth: int32 [512], replicated, may hold values from 0 to 63
- source_cell: int32 [512], replicated, may hold values from 0 to 32767
- receiver_depth: int32 [4096], replicated, may hold values from 0 to 63
- receiver_cell: int32 [4096], replicated, may hold values from 0 to 32767
- residual_traces: float32 [4, 2, 4096], P('shots'), may hold values from -5 to 5
Outputs:
- forward_older: float32 [4, 64, 128, 256], P('shots', 'depth')
- forward_newer: float32 [4, 64, 128, 256], P('shots', 'depth')
- adjoint_older: float32 [4, 64, 128, 256], P('shots', 'depth')
- adjoint_newer: float32 [4, 64, 128, 256], P('shots', 'depth')
- gradient: float32 [64, 128, 256], P(None, ('shots', 'depth'))
The draws below stay inside these ranges and needn't reach their ends.
All inputs are finite; a program needn't handle non-finite values.
Results may differ from the reference program's by a relative error of at most 0.00002.
Values sent between devices are 32-bit elements; how exact they have to be, the bound alone decides.
No kernel may reach another device: no remote copies, remote signals or barrier semaphores. Data moves between devices by JAX's collectives and lax.ppermute only.
A program may use at most 128 MiB of HBM per device.

```python
import jax
import jax.numpy as jnp
from jax import lax

NX = 128
NY = 256
STEPS = 2
NSRC = 512
NREC = 4096
NZ = 64
SUPER = 4


def set_ends(entries, rng, smallest, largest):
    spot = [jax.random.randint(jax.random.fold_in(rng, axis), (), 0, length) for axis, length in enumerate(entries.shape)]
    main_axis = entries.shape.index(max(entries.shape))
    beside = spot[:main_axis] + [(spot[main_axis] + 1) % entries.shape[main_axis]] + spot[main_axis + 1:]
    return entries.at[tuple(spot)].set(smallest).at[tuple(beside)].set(largest)


def level_of(rng, shape, pieces, least, top_value):
    def one(position, blocks):
        draws = jax.random.uniform(jax.random.fold_in(jax.random.fold_in(rng, 6), position), (blocks,), jnp.float32, least / len(pieces), top_value / len(pieces))
        return jnp.repeat(jnp.exp(draws), shape[position] // blocks).reshape((-1,) + (1,) * (len(shape) - position - 1))

    loudness = one(*pieces[0])
    for cut in pieces[1:]:
        loudness = loudness * one(*cut)
    return loudness


def scatter_about(rng, extent, scale, limit, cuts=(), kind=jnp.bfloat16):
    values = jax.random.normal(rng, extent, jnp.float32) * scale
    if len(cuts) > 0:
        values = level_of(rng, extent, cuts, -0.22, 0.18) * values
    return jnp.clip(values, min=-limit, max=limit).astype(kind)


def setup_inputs(seed: int = 0) -> dict:
    splits = jax.random.split(jax.random.key(seed), 13)
    forward_prev = scatter_about(splits[0], (SUPER, NZ, NX, NY), 0.5, 3.0, ((0, 4), (1, 8)), jnp.float32)
    forward_now = scatter_about(splits[1], (SUPER, NZ, NX, NY), 0.5, 3.0, ((0, 4), (1, 8)), jnp.float32)
    adjoint_prev = scatter_about(splits[2], (SUPER, NZ, NX, NY), 0.5, 3.0, ((0, 4), (1, 8)), jnp.float32)
    adjoint_now = scatter_about(splits[3], (SUPER, NZ, NX, NY), 0.5, 3.0, ((0, 4), (1, 8)), jnp.float32)
    courant = jnp.clip(0.05 + 0.13000001 * jax.random.uniform(splits[4], (NZ, NX, NY), jnp.float32) ** level_of(splits[4], (NZ, NX, NY), ((0, 8),), -0.2, 0.2), 0.05, 0.18)
    wavelet = scatter_about(splits[5], (STEPS, NSRC), 1.0, 5.0, (), jnp.float32)
    sign_bits = set_ends(jax.random.randint(splits[6], (SUPER, NSRC), 0, 2), jax.random.fold_in(splits[6], 1), 0, 1).astype(jnp.int32)
    source_depth = set_ends(jax.random.randint(splits[7], (NSRC,), 0, NZ), jax.random.fold_in(splits[7], 1), 0, NZ - 1).astype(jnp.int32)
    source_cell = set_ends(jax.random.randint(splits[8], (NSRC,), 0, NX * NY), jax.random.fold_in(splits[8], 1), 0, (NX * NY) - 1).astype(jnp.int32)
    receiver_depth = set_ends(jax.random.randint(splits[9], (NREC,), 0, NZ), jax.random.fold_in(splits[9], 1), 0, NZ - 1).astype(jnp.int32)
    receiver_cell = set_ends(jax.random.randint(splits[10], (NREC,), 0, NX * NY), jax.random.fold_in(splits[10], 1), 0, (NX * NY) - 1).astype(jnp.int32)
    residual_traces = scatter_about(splits[11], (SUPER, STEPS, NREC), 1.0, 5.0, ((0, 4),), jnp.float32)
    return {"forward_prev": forward_prev, "forward_now": forward_now, "adjoint_prev": adjoint_prev, "adjoint_now": adjoint_now, "courant": courant, "wavelet": wavelet, "sign_bits": sign_bits, "source_depth": source_depth, "source_cell": source_cell, "receiver_depth": receiver_depth, "receiver_cell": receiver_cell, "residual_traces": residual_traces}


COEFFS = (-205.0 / 72.0, 8.0 / 5.0, -1.0 / 5.0, 8.0 / 315.0, -1.0 / 560.0)
KERNEL = (1.0 / 16.0, 4.0 / 16.0, 6.0 / 16.0, 4.0 / 16.0, 1.0 / 16.0)


def shifted(values, axis, offset):
    size = values.shape[axis]
    width = abs(offset)
    filler = jnp.zeros_like(lax.slice_in_dim(values, 0, width, axis=axis))
    if offset > 0:
        kept = lax.slice_in_dim(values, offset, size, axis=axis)
        return jnp.concatenate([kept, filler], axis=axis)
    kept = lax.slice_in_dim(values, 0, size - width, axis=axis)
    return jnp.concatenate([filler, kept], axis=axis)


def laplace(extended):
    zaxis = extended.ndim - 3
    planes = extended.shape[zaxis] - 8
    core = lax.slice_in_dim(extended, 4, 4 + planes, axis=zaxis)
    total = (3.0 * COEFFS[0]) * core
    for k in range(1, 5):
        near = lax.slice_in_dim(extended, 4 + k, 4 + k + planes, axis=zaxis) + lax.slice_in_dim(extended, 4 - k, 4 - k + planes, axis=zaxis)
        near = near + shifted(core, zaxis + 1, k) + shifted(core, zaxis + 1, -k)
        near = near + shifted(core, zaxis + 2, k) + shifted(core, zaxis + 2, -k)
        total = total + COEFFS[k] * near
    return total


def smooth(values, axis):
    total = KERNEL[2] * values
    for k in (1, 2):
        total = total + KERNEL[2 + k] * (shifted(values, axis, k) + shifted(values, axis, -k))
    return total


def reference(forward_prev, forward_now, adjoint_prev, adjoint_now, courant, wavelet, sign_bits, source_depth, source_cell, receiver_depth, receiver_cell, residual_traces):
    lateral = NX * NY
    source_flat = (source_depth * lateral + source_cell).astype(jnp.int32)
    receiver_flat = (receiver_depth * lateral + receiver_cell).astype(jnp.int32)
    signs = (2 * sign_bits - 1).astype(jnp.float32)

    def spread(flat, values):
        grid = jnp.zeros((NZ * lateral,), jnp.float32).at[flat].add(values)
        return grid.reshape(NZ, NX, NY)

    def advance(total, inputs):
        f_prev, f_now, a_prev, a_now, sign_row, traces = inputs
        for step in range(STEPS):
            f_ext = jnp.pad(f_now, ((4, 4), (0, 0), (0, 0)))
            a_ext = jnp.pad(a_now, ((4, 4), (0, 0), (0, 0)))
            f_new = 2.0 * f_now - f_prev + courant * laplace(f_ext) + spread(source_flat, sign_row * wavelet[step])
            a_new = 2.0 * a_now - a_prev + courant * laplace(a_ext) + spread(receiver_flat, traces[step])
            total = total + f_new * a_new
            f_prev, f_now = f_now, f_new
            a_prev, a_now = a_now, a_new
        return total, (f_prev, f_now, a_prev, a_now)

    start = jnp.zeros((NZ, NX, NY), jnp.float32)
    total, fields = lax.scan(advance, start, (forward_prev, forward_now, adjoint_prev, adjoint_now, signs, residual_traces))
    gradient = smooth(smooth(smooth(total, 1), 2), 0)
    return fields[0], fields[1], fields[2], fields[3], gradient
```

```python
import jax
import jax.numpy as jnp
from jax import lax
from jax.sharding import PartitionSpec as P

STEPS = 2
HALO = 4


COEFFS = (-205.0 / 72.0, 8.0 / 5.0, -1.0 / 5.0, 8.0 / 315.0, -1.0 / 560.0)
KERNEL = (1.0 / 16.0, 4.0 / 16.0, 6.0 / 16.0, 4.0 / 16.0, 1.0 / 16.0)


def shifted(values, axis, offset):
    size = values.shape[axis]
    width = abs(offset)
    pads = [(0, 0, 0)] * values.ndim
    if offset > 0:
        kept = lax.slice_in_dim(values, offset, size, axis=axis)
        pads[axis] = (0, width, 0)
    else:
        kept = lax.slice_in_dim(values, 0, size - width, axis=axis)
        pads[axis] = (width, 0, 0)
    return lax.pad(kept, jnp.array(0.0, values.dtype), pads)


def local_laplace(core, zaxis):
    total = 3.0 * COEFFS[0] * core
    for k in range(1, 5):
        near = shifted(core, zaxis, k) + shifted(core, zaxis, -k)
        near = near + shifted(core, zaxis + 1, k) + shifted(core, zaxis + 1, -k)
        near = near + shifted(core, zaxis + 2, k) + shifted(core, zaxis + 2, -k)
        total = total + COEFFS[k] * near
    return total


def halo_laplace(below, above, planes, zaxis):
    parts = []
    for p in range(planes):
        term = None
        for k in range(1, 5):
            for q in (p - k, p + k):
                if q < 0:
                    piece = lax.index_in_dim(below, HALO + q, axis=zaxis, keepdims=True)
                elif q >= planes:
                    piece = lax.index_in_dim(above, q - planes, axis=zaxis, keepdims=True)
                else:
                    continue
                piece = COEFFS[k] * piece
                term = piece if term is None else term + piece
        parts.append(term)
    return jnp.concatenate(parts, axis=zaxis)


def smooth(values, axis):
    total = KERNEL[2] * values
    for k in (1, 2):
        total = total + KERNEL[2 + k] * (shifted(values, axis, k) + shifted(values, axis, -k))
    return total


def exchange(current, dim):
    devices = lax.axis_size("depth")
    length = current.shape[dim]
    up = [(i, i + 1) for i in range(devices - 1)]
    down = [(i + 1, i) for i in range(devices - 1)]
    last = lax.slice_in_dim(current, length - HALO, length, axis=dim)
    leading = lax.slice_in_dim(current, 0, HALO, axis=dim)
    below = lax.ppermute(last, "depth", up)
    above = lax.ppermute(leading, "depth", down)
    return below, above


def spread_all(source_flat, receiver_flat, source_values, receiver_values, first_plane, planes, rows, cols):
    lateral = rows * cols
    limit = planes * lateral
    total = 2 * limit

    def local_of(flat, field):
        local = flat - first_plane * lateral
        inside = (local >= 0) & (local < limit)
        return jnp.where(inside, local + field * limit, total)

    index = jnp.concatenate([local_of(source_flat, 0), local_of(receiver_flat, 1)])
    values = jnp.concatenate([source_values, receiver_values], axis=1)
    grid = jnp.zeros((values.shape[0], total), jnp.float32).at[:, index].add(values, mode="drop")
    return grid.reshape(values.shape[0], 2, 1, planes, rows, cols)


def on_device(
    forward_prev,
    forward_now,
    adjoint_prev,
    adjoint_now,
    courant,
    wavelet,
    sign_bits,
    source_depth,
    source_cell,
    receiver_depth,
    receiver_cell,
    residual_traces,
):
    planes, rows, cols = courant.shape
    lateral = rows * cols
    source_flat = source_depth * lateral + source_cell
    receiver_flat = receiver_depth * lateral + receiver_cell
    signs = (2 * sign_bits - 1).astype(jnp.float32)
    position = lax.axis_index("depth")
    earlier = jnp.stack([forward_prev, adjoint_prev])
    current = jnp.stack([forward_now, adjoint_now])
    zaxis = 2
    below, above = exchange(current, zaxis)
    terms = spread_all(
        source_flat,
        receiver_flat,
        signs[0][None, :] * wavelet,
        residual_traces[0],
        position * planes,
        planes,
        rows,
        cols,
    )
    reduced = None
    for step in range(STEPS):
        base = 2.0 * current - earlier + courant * local_laplace(current, zaxis) + terms[step]
        fresh = base + courant * halo_laplace(below, above, planes, zaxis)
        if step + 1 < STEPS:
            below, above = exchange(fresh, zaxis)
        part = smooth(smooth(fresh[0, 0] * fresh[1, 0], 1), 2)
        part = lax.psum_scatter(part, "shots", scatter_dimension=1, tiled=True)
        reduced = part if reduced is None else reduced + part
        earlier, current = (current, fresh)
    columns = lax.all_to_all(reduced, "depth", split_axis=1, concat_axis=0, tiled=True)
    gradient = smooth(columns, 0)
    return (earlier[0], current[0], earlier[1], current[1], gradient)


def solution(mesh):
    in_specs = (
        P("shots", "depth", None, None),
        P("shots", "depth", None, None),
        P("shots", "depth", None, None),
        P("shots", "depth", None, None),
        P("depth", None, None),
        P(),
        P("shots", None),
        P(),
        P(),
        P(),
        P(),
        P("shots", None, None),
    )
    out_specs = (
        P("shots", "depth", None, None),
        P("shots", "depth", None, None),
        P("shots", "depth", None, None),
        P("shots", "depth", None, None),
        P(None, ("shots", "depth"), None),
    )
    return jax.shard_map(
        on_device, mesh=mesh, in_specs=in_specs, out_specs=out_specs, check_vma=False
    )
```

```python
import jax
import jax.numpy as jnp
from jax import lax
from jax.sharding import PartitionSpec as P

STEPS = 2
HALO = 4


COEFFS = (-205.0 / 72.0, 8.0 / 5.0, -1.0 / 5.0, 8.0 / 315.0, -1.0 / 560.0)
KERNEL = (1.0 / 16.0, 4.0 / 16.0, 6.0 / 16.0, 4.0 / 16.0, 1.0 / 16.0)


def shifted(values, axis, offset):
    size = values.shape[axis]
    width = abs(offset)
    pads = [(0, 0, 0)] * values.ndim
    if offset > 0:
        kept = lax.slice_in_dim(values, offset, size, axis=axis)
        pads[axis] = (0, width, 0)
    else:
        kept = lax.slice_in_dim(values, 0, size - width, axis=axis)
        pads[axis] = (width, 0, 0)
    return lax.pad(kept, jnp.array(0.0, values.dtype), pads)


def band(size):
    index = jnp.arange(size)
    gap = jnp.abs(index[:, None] - index[None, :])
    matrix = jnp.zeros((size, size), jnp.float32)
    for k in range(1, 5):
        matrix = jnp.where(gap == k, jnp.float32(COEFFS[k]), matrix)
    return matrix


def local_laplace(core, zaxis):
    rows, cols = core.shape[zaxis + 1], core.shape[zaxis + 2]
    high = lax.Precision.HIGHEST
    along_y = jnp.einsum("...xy,yk->...xk", core, band(cols), precision=high)
    along_x = jnp.einsum("...xy,kx->...ky", core, band(rows), precision=high)
    total = 3.0 * COEFFS[0] * core + (along_x + along_y)
    for k in range(1, 5):
        near = shifted(core, zaxis, k) + shifted(core, zaxis, -k)
        total = total + COEFFS[k] * near
    return total


def halo_laplace(below, above, planes, zaxis):
    parts = []
    for p in range(planes):
        term = None
        for k in range(1, 5):
            for q in (p - k, p + k):
                if q < 0:
                    piece = lax.index_in_dim(below, HALO + q, axis=zaxis, keepdims=True)
                elif q >= planes:
                    piece = lax.index_in_dim(above, q - planes, axis=zaxis, keepdims=True)
                else:
                    continue
                piece = COEFFS[k] * piece
                term = piece if term is None else term + piece
        parts.append(term)
    return jnp.concatenate(parts, axis=zaxis)


def smooth(values, axis):
    total = KERNEL[2] * values
    for k in (1, 2):
        total = total + KERNEL[2 + k] * (shifted(values, axis, k) + shifted(values, axis, -k))
    return total


def exchange(current, dim):
    devices = lax.axis_size("depth")
    length = current.shape[dim]
    up = [(i, i + 1) for i in range(devices - 1)]
    down = [(i + 1, i) for i in range(devices - 1)]
    last = lax.slice_in_dim(current, length - HALO, length, axis=dim)
    leading = lax.slice_in_dim(current, 0, HALO, axis=dim)
    below = lax.ppermute(last, "depth", up)
    above = lax.ppermute(leading, "depth", down)
    return below, above


def spread(flat, values, first_plane, planes, rows, cols):
    lateral = rows * cols
    limit = planes * lateral
    local = flat - first_plane * lateral
    local = jnp.where((local >= 0) & (local < limit), local, limit)
    grid = jnp.zeros((values.shape[0], limit), jnp.float32).at[:, local].add(values, mode="drop")
    return grid.reshape(values.shape[0], planes, rows, cols)


def reduce_shots(values, dim):
    devices = lax.axis_size("shots")
    me = lax.axis_index("shots")
    length = values.shape[dim]
    shape = values.shape
    blocks = values.reshape(shape[:dim] + (devices, length // devices) + shape[dim + 1 :])
    bit = 1
    while bit < devices:
        count = blocks.shape[dim]
        paired = blocks.reshape(shape[:dim] + (count // 2, 2, length // devices) + shape[dim + 1 :])
        mine = (me // bit) % 2
        keep = lax.dynamic_index_in_dim(paired, mine, axis=dim + 1, keepdims=False)
        send = lax.dynamic_index_in_dim(paired, 1 - mine, axis=dim + 1, keepdims=False)
        pairs = [(i, i ^ bit) for i in range(devices)]
        blocks = keep + lax.ppermute(send, "shots", pairs)
        bit *= 2
    return blocks.reshape(shape[:dim] + (length // devices,) + shape[dim + 1 :])


def on_device(
    forward_prev,
    forward_now,
    adjoint_prev,
    adjoint_now,
    courant,
    wavelet,
    sign_bits,
    source_depth,
    source_cell,
    receiver_depth,
    receiver_cell,
    residual_traces,
):
    planes, rows, cols = courant.shape
    lateral = rows * cols
    source_flat = source_depth * lateral + source_cell
    receiver_flat = receiver_depth * lateral + receiver_cell
    signs = (2 * sign_bits - 1).astype(jnp.float32)
    position = lax.axis_index("depth")
    earlier = jnp.stack([forward_prev, adjoint_prev])
    current = jnp.stack([forward_now, adjoint_now])
    zaxis = 2
    below, above = exchange(current, zaxis)
    first_plane = position * planes
    correlation = None
    for step in range(STEPS):
        forward_part = spread(source_flat, signs * wavelet[step][None, :], first_plane, planes, rows, cols)
        adjoint_part = spread(receiver_flat, residual_traces[:, step, :], first_plane, planes, rows, cols)
        terms = jnp.stack([forward_part, adjoint_part])
        base = 2.0 * current - earlier + courant * local_laplace(current, zaxis) + terms
        fresh = base + courant * halo_laplace(below, above, planes, zaxis)
        if step + 1 < STEPS:
            below, above = exchange(fresh, zaxis)
        part = fresh[0, 0] * fresh[1, 0]
        correlation = part if correlation is None else correlation + part
        earlier, current = (current, fresh)
    lateral_smooth = smooth(smooth(correlation, 1), 2)
    reduced = reduce_shots(lateral_smooth, 1)
    columns = lax.all_to_all(reduced, "depth", split_axis=1, concat_axis=0, tiled=True)
    gradient = smooth(columns, 0)
    return (earlier[0], current[0], earlier[1], current[1], gradient)


def solution(mesh):
    in_specs = (
        P("shots", "depth", None, None),
        P("shots", "depth", None, None),
        P("shots", "depth", None, None),
        P("shots", "depth", None, None),
        P("depth", None, None),
        P(),
        P("shots", None),
        P(),
        P(),
        P(),
        P(),
        P("shots", None, None),
    )
    out_specs = (
        P("shots", "depth", None, None),
        P("shots", "depth", None, None),
        P("shots", "depth", None, None),
        P("shots", "depth", None, None),
        P(None, ("shots", "depth"), None),
    )
    return jax.shard_map(
        on_device, mesh=mesh, in_specs=in_specs, out_specs=out_specs, check_vma=False
    )
```

```python
import jax
import jax.numpy as jnp
from jax import lax
from jax.sharding import PartitionSpec as P

STEPS = 2
HALO = 4


COEFFS = (-205.0 / 72.0, 8.0 / 5.0, -1.0 / 5.0, 8.0 / 315.0, -1.0 / 560.0)
KERNEL = (1.0 / 16.0, 4.0 / 16.0, 6.0 / 16.0, 4.0 / 16.0, 1.0 / 16.0)


def shifted(values, axis, offset):
    size = values.shape[axis]
    width = abs(offset)
    pads = [(0, 0, 0)] * values.ndim
    if offset > 0:
        kept = lax.slice_in_dim(values, offset, size, axis=axis)
        pads[axis] = (0, width, 0)
    else:
        kept = lax.slice_in_dim(values, 0, size - width, axis=axis)
        pads[axis] = (width, 0, 0)
    return lax.pad(kept, jnp.array(0.0, values.dtype), pads)


def band(size):
    index = jnp.arange(size)
    gap = jnp.abs(index[:, None] - index[None, :])
    matrix = jnp.zeros((size, size), jnp.float32)
    for k in range(1, 5):
        matrix = jnp.where(gap == k, jnp.float32(COEFFS[k]), matrix)
    return matrix


def local_laplace(core, zaxis):
    rows, cols = core.shape[zaxis + 1], core.shape[zaxis + 2]
    high = lax.Precision.HIGHEST
    along_y = jnp.einsum("...xy,yk->...xk", core, band(cols), precision=high)
    along_x = jnp.einsum("...xy,kx->...ky", core, band(rows), precision=high)
    total = 3.0 * COEFFS[0] * core + (along_x + along_y)
    for k in range(1, 5):
        near = shifted(core, zaxis, k) + shifted(core, zaxis, -k)
        total = total + COEFFS[k] * near
    return total


def halo_laplace(below, above, planes, zaxis):
    parts = []
    for p in range(planes):
        term = None
        for k in range(1, 5):
            for q in (p - k, p + k):
                if q < 0:
                    piece = lax.index_in_dim(below, HALO + q, axis=zaxis, keepdims=True)
                elif q >= planes:
                    piece = lax.index_in_dim(above, q - planes, axis=zaxis, keepdims=True)
                else:
                    continue
                piece = COEFFS[k] * piece
                term = piece if term is None else term + piece
        parts.append(term)
    return jnp.concatenate(parts, axis=zaxis)


def smooth(values, axis):
    total = KERNEL[2] * values
    for k in (1, 2):
        total = total + KERNEL[2 + k] * (shifted(values, axis, k) + shifted(values, axis, -k))
    return total


def exchange(current, dim):
    devices = lax.axis_size("depth")
    length = current.shape[dim]
    up = [(i, i + 1) for i in range(devices - 1)]
    down = [(i + 1, i) for i in range(devices - 1)]
    last = lax.slice_in_dim(current, length - HALO, length, axis=dim)
    leading = lax.slice_in_dim(current, 0, HALO, axis=dim)
    below = lax.ppermute(last, "depth", up)
    above = lax.ppermute(leading, "depth", down)
    return below, above


def spread(flat, values, first_plane, planes, rows, cols):
    lateral = rows * cols
    limit = planes * lateral
    local = flat - first_plane * lateral
    local = jnp.where((local >= 0) & (local < limit), local, limit)
    grid = jnp.zeros((values.shape[0], limit), jnp.float32).at[:, local].add(values, mode="drop")
    return grid.reshape(values.shape[0], planes, rows, cols)


def reduce_shots(values, dim):
    devices = lax.axis_size("shots")
    me = lax.axis_index("shots")
    length = values.shape[dim]
    shape = values.shape
    blocks = values.reshape(shape[:dim] + (devices, length // devices) + shape[dim + 1 :])
    bit = 1
    while bit < devices:
        count = blocks.shape[dim]
        paired = blocks.reshape(shape[:dim] + (count // 2, 2, length // devices) + shape[dim + 1 :])
        mine = (me // bit) % 2
        keep = lax.dynamic_index_in_dim(paired, mine, axis=dim + 1, keepdims=False)
        send = lax.dynamic_index_in_dim(paired, 1 - mine, axis=dim + 1, keepdims=False)
        pairs = [(i, i ^ bit) for i in range(devices)]
        blocks = keep + lax.ppermute(send, "shots", pairs)
        bit *= 2
    return blocks.reshape(shape[:dim] + (length // devices,) + shape[dim + 1 :])


def on_device(
    forward_prev,
    forward_now,
    adjoint_prev,
    adjoint_now,
    courant,
    wavelet,
    sign_bits,
    source_depth,
    source_cell,
    receiver_depth,
    receiver_cell,
    residual_traces,
):
    planes, rows, cols = courant.shape
    lateral = rows * cols
    source_flat = source_depth * lateral + source_cell
    receiver_flat = receiver_depth * lateral + receiver_cell
    signs = (2 * sign_bits - 1).astype(jnp.float32)
    position = lax.axis_index("depth")
    earlier = jnp.stack([forward_prev, adjoint_prev])
    current = jnp.stack([forward_now, adjoint_now])
    zaxis = 2
    below, above = exchange(current, zaxis)
    first_plane = position * planes
    correlation = None
    gate = ()
    for step in range(STEPS):
        if step > 0:
            gate, (source_flat, receiver_flat, signs, wavelet, residual_traces) = lax.optimization_barrier(
                (gate, (source_flat, receiver_flat, signs, wavelet, residual_traces))
            )
        forward_part = spread(source_flat, signs * wavelet[step][None, :], first_plane, planes, rows, cols)
        adjoint_part = spread(receiver_flat, residual_traces[:, step, :], first_plane, planes, rows, cols)
        terms = jnp.stack([forward_part, adjoint_part])
        base = 2.0 * current - earlier + courant * local_laplace(current, zaxis) + terms
        fresh = base + courant * halo_laplace(below, above, planes, zaxis)
        if step + 1 < STEPS:
            below, above = exchange(fresh, zaxis)
            gate = fresh
        part = fresh[0, 0] * fresh[1, 0]
        correlation = part if correlation is None else correlation + part
        earlier, current = (current, fresh)
    lateral_smooth = smooth(smooth(correlation, 1), 2)
    reduced = reduce_shots(lateral_smooth, 1)
    columns = lax.all_to_all(reduced, "depth", split_axis=1, concat_axis=0, tiled=True)
    gradient = smooth(columns, 0)
    return (earlier[0], current[0], earlier[1], current[1], gradient)


def solution(mesh):
    in_specs = (
        P("shots", "depth", None, None),
        P("shots", "depth", None, None),
        P("shots", "depth", None, None),
        P("shots", "depth", None, None),
        P("depth", None, None),
        P(),
        P("shots", None),
        P(),
        P(),
        P(),
        P(),
        P("shots", None, None),
    )
    out_specs = (
        P("shots", "depth", None, None),
        P("shots", "depth", None, None),
        P("shots", "depth", None, None),
        P("shots", "depth", None, None),
        P(None, ("shots", "depth"), None),
    )
    return jax.shard_map(
        on_device, mesh=mesh, in_specs=in_specs, out_specs=out_specs, check_vma=False
    )
```

```python
import jax
import jax.numpy as jnp
from jax import lax
from jax.sharding import PartitionSpec as P

STEPS = 2
HALO = 4


COEFFS = (-205.0 / 72.0, 8.0 / 5.0, -1.0 / 5.0, 8.0 / 315.0, -1.0 / 560.0)
KERNEL = (1.0 / 16.0, 4.0 / 16.0, 6.0 / 16.0, 4.0 / 16.0, 1.0 / 16.0)


def shifted(values, axis, offset):
    size = values.shape[axis]
    width = abs(offset)
    pads = [(0, 0, 0)] * values.ndim
    if offset > 0:
        kept = lax.slice_in_dim(values, offset, size, axis=axis)
        pads[axis] = (0, width, 0)
    else:
        kept = lax.slice_in_dim(values, 0, size - width, axis=axis)
        pads[axis] = (width, 0, 0)
    return lax.pad(kept, jnp.array(0.0, values.dtype), pads)


def band(size):
    index = jnp.arange(size)
    gap = jnp.abs(index[:, None] - index[None, :])
    matrix = jnp.zeros((size, size), jnp.float32)
    for k in range(1, 5):
        matrix = jnp.where(gap == k, jnp.float32(COEFFS[k]), matrix)
    return matrix


def lateral_laplace(core, zaxis):
    rows, cols = core.shape[zaxis + 1], core.shape[zaxis + 2]
    high = lax.Precision.HIGHEST
    along_y = jnp.einsum("...xy,yk->...xk", core, band(cols), precision=high)
    along_x = jnp.einsum("...xy,kx->...ky", core, band(rows), precision=high)
    return 3.0 * COEFFS[0] * core + (along_x + along_y)


def depth_laplace(below, core, above, zaxis):
    planes = core.shape[zaxis]
    extended = jnp.concatenate([below, core, above], axis=zaxis)
    total = None
    for k in range(1, 5):
        near = lax.slice_in_dim(extended, HALO + k, HALO + k + planes, axis=zaxis) + lax.slice_in_dim(
            extended, HALO - k, HALO - k + planes, axis=zaxis
        )
        total = COEFFS[k] * near if total is None else total + COEFFS[k] * near
    return total


def smooth(values, axis):
    total = KERNEL[2] * values
    for k in (1, 2):
        total = total + KERNEL[2 + k] * (shifted(values, axis, k) + shifted(values, axis, -k))
    return total


def exchange(current, dim):
    devices = lax.axis_size("depth")
    length = current.shape[dim]
    up = [(i, i + 1) for i in range(devices - 1)]
    down = [(i + 1, i) for i in range(devices - 1)]
    last = lax.slice_in_dim(current, length - HALO, length, axis=dim)
    leading = lax.slice_in_dim(current, 0, HALO, axis=dim)
    below = lax.ppermute(last, "depth", up)
    above = lax.ppermute(leading, "depth", down)
    return below, above


def spread(flat, values, first_plane, planes, rows, cols):
    lateral = rows * cols
    limit = planes * lateral
    local = flat - first_plane * lateral
    local = jnp.where((local >= 0) & (local < limit), local, limit)
    grid = jnp.zeros((values.shape[0], limit), jnp.float32).at[:, local].add(values, mode="drop")
    return grid.reshape(values.shape[0], planes, rows, cols)


def reduce_shots(values, dim):
    devices = lax.axis_size("shots")
    me = lax.axis_index("shots")
    length = values.shape[dim]
    shape = values.shape
    blocks = values.reshape(shape[:dim] + (devices, length // devices) + shape[dim + 1 :])
    bit = 1
    while bit < devices:
        count = blocks.shape[dim]
        paired = blocks.reshape(shape[:dim] + (count // 2, 2, length // devices) + shape[dim + 1 :])
        mine = (me // bit) % 2
        keep = lax.dynamic_index_in_dim(paired, mine, axis=dim + 1, keepdims=False)
        send = lax.dynamic_index_in_dim(paired, 1 - mine, axis=dim + 1, keepdims=False)
        pairs = [(i, i ^ bit) for i in range(devices)]
        blocks = keep + lax.ppermute(send, "shots", pairs)
        bit *= 2
    return blocks.reshape(shape[:dim] + (length // devices,) + shape[dim + 1 :])


def on_device(
    forward_prev,
    forward_now,
    adjoint_prev,
    adjoint_now,
    courant,
    wavelet,
    sign_bits,
    source_depth,
    source_cell,
    receiver_depth,
    receiver_cell,
    residual_traces,
):
    planes, rows, cols = courant.shape
    lateral = rows * cols
    source_flat = source_depth * lateral + source_cell
    receiver_flat = receiver_depth * lateral + receiver_cell
    signs = (2 * sign_bits - 1).astype(jnp.float32)
    position = lax.axis_index("depth")
    earlier = jnp.stack([forward_prev, adjoint_prev])
    current = jnp.stack([forward_now, adjoint_now])
    zaxis = 2
    below, above = exchange(current, zaxis)
    first_plane = position * planes
    correlation = None
    gate = ()
    for step in range(STEPS):
        if step > 0:
            gate, (source_flat, receiver_flat, signs, wavelet, residual_traces) = lax.optimization_barrier(
                (gate, (source_flat, receiver_flat, signs, wavelet, residual_traces))
            )
        forward_part = spread(source_flat, signs * wavelet[step][None, :], first_plane, planes, rows, cols)
        adjoint_part = spread(receiver_flat, residual_traces[:, step, :], first_plane, planes, rows, cols)
        terms = jnp.stack([forward_part, adjoint_part])
        lateral_part = lateral_laplace(current, zaxis)
        fresh = (
            2.0 * current
            - earlier
            + courant * (lateral_part + depth_laplace(below, current, above, zaxis))
            + terms
        )
        if step + 1 < STEPS:
            below, above = exchange(fresh, zaxis)
            gate = fresh
        part = fresh[0, 0] * fresh[1, 0]
        correlation = part if correlation is None else correlation + part
        earlier, current = (current, fresh)
    lateral_smooth = smooth(smooth(correlation, 1), 2)
    reduced = reduce_shots(lateral_smooth, 1)
    columns = lax.all_to_all(reduced, "depth", split_axis=1, concat_axis=0, tiled=True)
    gradient = smooth(columns, 0)
    return (earlier[0], current[0], earlier[1], current[1], gradient)


def solution(mesh):
    in_specs = (
        P("shots", "depth", None, None),
        P("shots", "depth", None, None),
        P("shots", "depth", None, None),
        P("shots", "depth", None, None),
        P("depth", None, None),
        P(),
        P("shots", None),
        P(),
        P(),
        P(),
        P(),
        P("shots", None, None),
    )
    out_specs = (
        P("shots", "depth", None, None),
        P("shots", "depth", None, None),
        P("shots", "depth", None, None),
        P("shots", "depth", None, None),
        P(None, ("shots", "depth"), None),
    )
    return jax.shard_map(
        on_device, mesh=mesh, in_specs=in_specs, out_specs=out_specs, check_vma=False
    )
```

```python
import jax
import jax.numpy as jnp
from jax import lax
from jax.sharding import PartitionSpec as P

STEPS = 2
HALO = 4


COEFFS = (-205.0 / 72.0, 8.0 / 5.0, -1.0 / 5.0, 8.0 / 315.0, -1.0 / 560.0)
KERNEL = (1.0 / 16.0, 4.0 / 16.0, 6.0 / 16.0, 4.0 / 16.0, 1.0 / 16.0)


def shifted(values, axis, offset):
    size = values.shape[axis]
    width = abs(offset)
    pads = [(0, 0, 0)] * values.ndim
    if offset > 0:
        kept = lax.slice_in_dim(values, offset, size, axis=axis)
        pads[axis] = (0, width, 0)
    else:
        kept = lax.slice_in_dim(values, 0, size - width, axis=axis)
        pads[axis] = (width, 0, 0)
    return lax.pad(kept, jnp.array(0.0, values.dtype), pads)


def band(size):
    index = jnp.arange(size)
    gap = jnp.abs(index[:, None] - index[None, :])
    matrix = jnp.zeros((size, size), jnp.float32)
    for k in range(1, 5):
        matrix = jnp.where(gap == k, jnp.float32(COEFFS[k]), matrix)
    return matrix


def lateral_laplace(core, zaxis):
    rows, cols = core.shape[zaxis + 1], core.shape[zaxis + 2]
    high = lax.Precision.HIGHEST
    along_y = jnp.einsum("...xy,yk->...xk", core, band(cols), precision=high)
    along_x = jnp.einsum("...xy,kx->...ky", core, band(rows), precision=high)
    return 3.0 * COEFFS[0] * core + (along_x + along_y)


def depth_laplace(below, core, above, zaxis):
    planes = core.shape[zaxis]
    extended = jnp.concatenate([below, core, above], axis=zaxis)
    total = None
    for k in range(1, 5):
        near = lax.slice_in_dim(extended, HALO + k, HALO + k + planes, axis=zaxis) + lax.slice_in_dim(
            extended, HALO - k, HALO - k + planes, axis=zaxis
        )
        total = COEFFS[k] * near if total is None else total + COEFFS[k] * near
    return total


def smooth(values, axis):
    total = KERNEL[2] * values
    for k in (1, 2):
        total = total + KERNEL[2 + k] * (shifted(values, axis, k) + shifted(values, axis, -k))
    return total


def exchange(current, dim):
    devices = lax.axis_size("depth")
    length = current.shape[dim]
    up = [(i, i + 1) for i in range(devices - 1)]
    down = [(i + 1, i) for i in range(devices - 1)]
    last = lax.slice_in_dim(current, length - HALO, length, axis=dim)
    leading = lax.slice_in_dim(current, 0, HALO, axis=dim)
    below = lax.ppermute(last, "depth", up)
    above = lax.ppermute(leading, "depth", down)
    return below, above


def spread(flat, values, first_plane, planes, rows, cols):
    lateral = rows * cols
    limit = planes * lateral
    local = flat - first_plane * lateral
    local = jnp.where((local >= 0) & (local < limit), local, limit)
    grid = jnp.zeros((values.shape[0], limit), jnp.float32).at[:, local].add(values, mode="drop")
    return grid.reshape(values.shape[0], planes, rows, cols)


def reduce_shots(values, dim):
    devices = lax.axis_size("shots")
    me = lax.axis_index("shots")
    length = values.shape[dim]
    shape = values.shape
    blocks = values.reshape(shape[:dim] + (devices, length // devices) + shape[dim + 1 :])
    bit = 1
    while bit < devices:
        count = blocks.shape[dim]
        paired = blocks.reshape(shape[:dim] + (count // 2, 2, length // devices) + shape[dim + 1 :])
        mine = (me // bit) % 2
        keep = lax.dynamic_index_in_dim(paired, mine, axis=dim + 1, keepdims=False)
        send = lax.dynamic_index_in_dim(paired, 1 - mine, axis=dim + 1, keepdims=False)
        pairs = [(i, i ^ bit) for i in range(devices)]
        blocks = keep + lax.ppermute(send, "shots", pairs)
        bit *= 2
    return blocks.reshape(shape[:dim] + (length // devices,) + shape[dim + 1 :])


def transpose_depth(values, dim):
    devices = lax.axis_size("depth")
    me = lax.axis_index("depth")
    shape = values.shape
    length = shape[dim] // devices
    chunks = values.reshape(shape[:dim] + (devices, length) + shape[dim + 1 :])
    parts = [None] * devices
    parts[0] = lax.dynamic_index_in_dim(chunks, me, axis=dim, keepdims=False)
    for offset in range(1, devices):
        send = lax.dynamic_index_in_dim(chunks, (me + offset) % devices, axis=dim, keepdims=False)
        pairs = [(i, (i + offset) % devices) for i in range(devices)]
        parts[devices - offset] = lax.ppermute(send, "depth", pairs)
    ordered = jnp.roll(jnp.stack(parts), me, axis=0)
    return ordered.reshape((devices * shape[0],) + ordered.shape[2:])


def on_device(
    forward_prev,
    forward_now,
    adjoint_prev,
    adjoint_now,
    courant,
    wavelet,
    sign_bits,
    source_depth,
    source_cell,
    receiver_depth,
    receiver_cell,
    residual_traces,
):
    planes, rows, cols = courant.shape
    lateral = rows * cols
    source_flat = source_depth * lateral + source_cell
    receiver_flat = receiver_depth * lateral + receiver_cell
    signs = (2 * sign_bits - 1).astype(jnp.float32)
    position = lax.axis_index("depth")
    earlier = jnp.stack([forward_prev, adjoint_prev])
    current = jnp.stack([forward_now, adjoint_now])
    zaxis = 2
    below, above = exchange(current, zaxis)
    first_plane = position * planes
    correlation = None
    gate = ()
    for step in range(STEPS):
        if step > 0:
            gate, (source_flat, receiver_flat, signs, wavelet, residual_traces) = lax.optimization_barrier(
                (gate, (source_flat, receiver_flat, signs, wavelet, residual_traces))
            )
        forward_part = spread(source_flat, signs * wavelet[step][None, :], first_plane, planes, rows, cols)
        adjoint_part = spread(receiver_flat, residual_traces[:, step, :], first_plane, planes, rows, cols)
        terms = jnp.stack([forward_part, adjoint_part])
        lateral_part = lateral_laplace(current, zaxis)
        fresh = (
            2.0 * current
            - earlier
            + courant * (lateral_part + depth_laplace(below, current, above, zaxis))
            + terms
        )
        if step + 1 < STEPS:
            below, above = exchange(fresh, zaxis)
            gate = fresh
        part = fresh[0, 0] * fresh[1, 0]
        correlation = part if correlation is None else correlation + part
        earlier, current = (current, fresh)
    lateral_smooth = smooth(smooth(correlation, 1), 2)
    reduced = reduce_shots(lateral_smooth, 1)
    columns = transpose_depth(reduced, 1)
    gradient = smooth(columns, 0)
    return (earlier[0], current[0], earlier[1], current[1], gradient)


def solution(mesh):
    in_specs = (
        P("shots", "depth", None, None),
        P("shots", "depth", None, None),
        P("shots", "depth", None, None),
        P("shots", "depth", None, None),
        P("depth", None, None),
        P(),
        P("shots", None),
        P(),
        P(),
        P(),
        P(),
        P("shots", None, None),
    )
    out_specs = (
        P("shots", "depth", None, None),
        P("shots", "depth", None, None),
        P("shots", "depth", None, None),
        P("shots", "depth", None, None),
        P(None, ("shots", "depth"), None),
    )
    return jax.shard_map(
        on_device, mesh=mesh, in_specs=in_specs, out_specs=out_specs, check_vma=False
    )
```

```python
import jax
import jax.numpy as jnp
from jax import lax
from jax.sharding import PartitionSpec as P

STEPS = 2
HALO = 4


COEFFS = (-205.0 / 72.0, 8.0 / 5.0, -1.0 / 5.0, 8.0 / 315.0, -1.0 / 560.0)
KERNEL = (1.0 / 16.0, 4.0 / 16.0, 6.0 / 16.0, 4.0 / 16.0, 1.0 / 16.0)


def shifted(values, axis, offset):
    size = values.shape[axis]
    width = abs(offset)
    pads = [(0, 0, 0)] * values.ndim
    if offset > 0:
        kept = lax.slice_in_dim(values, offset, size, axis=axis)
        pads[axis] = (0, width, 0)
    else:
        kept = lax.slice_in_dim(values, 0, size - width, axis=axis)
        pads[axis] = (width, 0, 0)
    return lax.pad(kept, jnp.array(0.0, values.dtype), pads)


def band(size):
    index = jnp.arange(size)
    gap = jnp.abs(index[:, None] - index[None, :])
    matrix = jnp.zeros((size, size), jnp.float32)
    for k in range(1, 5):
        matrix = jnp.where(gap == k, jnp.float32(COEFFS[k]), matrix)
    return matrix


def lateral_laplace(core, zaxis):
    rows, cols = core.shape[zaxis + 1], core.shape[zaxis + 2]
    high = lax.Precision.HIGHEST
    along_y = jnp.einsum("...xy,yk->...xk", core, band(cols), precision=high)
    along_x = jnp.einsum("...xy,kx->...ky", core, band(rows), precision=high)
    return 3.0 * COEFFS[0] * core + (along_x + along_y)


def depth_laplace(below, core, above, zaxis):
    planes = core.shape[zaxis]
    extended = jnp.concatenate([below, core, above], axis=zaxis)
    total = None
    for k in range(1, 5):
        near = lax.slice_in_dim(extended, HALO + k, HALO + k + planes, axis=zaxis) + lax.slice_in_dim(
            extended, HALO - k, HALO - k + planes, axis=zaxis
        )
        total = COEFFS[k] * near if total is None else total + COEFFS[k] * near
    return total


def smooth(values, axis):
    total = KERNEL[2] * values
    for k in (1, 2):
        total = total + KERNEL[2 + k] * (shifted(values, axis, k) + shifted(values, axis, -k))
    return total


def exchange(current, dim):
    devices = lax.axis_size("depth")
    length = current.shape[dim]
    up = [(i, i + 1) for i in range(devices - 1)]
    down = [(i + 1, i) for i in range(devices - 1)]
    last = lax.slice_in_dim(current, length - HALO, length, axis=dim)
    leading = lax.slice_in_dim(current, 0, HALO, axis=dim)
    below = lax.ppermute(last, "depth", up)
    above = lax.ppermute(leading, "depth", down)
    return below, above


def spread(flat, values, first_plane, planes, rows, cols):
    lateral = rows * cols
    limit = planes * lateral
    local = flat - first_plane * lateral
    local = jnp.where((local >= 0) & (local < limit), local, limit)
    grid = jnp.zeros((values.shape[0], limit), jnp.float32).at[:, local].add(values, mode="drop")
    return grid.reshape(values.shape[0], planes, rows, cols)


def reduce_shots(values, dim):
    devices = lax.axis_size("shots")
    me = lax.axis_index("shots")
    length = values.shape[dim]
    shape = values.shape
    blocks = values.reshape(shape[:dim] + (devices, length // devices) + shape[dim + 1 :])
    bit = 1
    while bit < devices:
        count = blocks.shape[dim]
        paired = blocks.reshape(shape[:dim] + (count // 2, 2, length // devices) + shape[dim + 1 :])
        mine = (me // bit) % 2
        keep = lax.dynamic_index_in_dim(paired, mine, axis=dim + 1, keepdims=False)
        send = lax.dynamic_index_in_dim(paired, 1 - mine, axis=dim + 1, keepdims=False)
        pairs = [(i, i ^ bit) for i in range(devices)]
        blocks = keep + lax.ppermute(send, "shots", pairs)
        bit *= 2
    return blocks.reshape(shape[:dim] + (length // devices,) + shape[dim + 1 :])


def local_part(field, prev, courant, term, zaxis):
    planes = field.shape[zaxis]
    along_z = jnp.einsum("zw,bwxy->bzxy", band(planes), field, precision=lax.Precision.HIGHEST)
    lateral = lateral_laplace(field, zaxis) + along_z
    return 2.0 * field - prev + courant * lateral + term


def edge_matrix(reach):
    index = jnp.arange(HALO)
    gap = index[:, None] + HALO - index[None, :]
    matrix = jnp.zeros((HALO, HALO), jnp.float32)
    for k in range(1, 5):
        matrix = jnp.where(gap == k, jnp.float32(COEFFS[k]), matrix)
    return matrix if reach < 0 else matrix[::-1, ::-1]


def edge_parts(pre, below, above, courant, zaxis):
    planes = pre.shape[zaxis]
    high_precision = lax.Precision.HIGHEST
    low = jnp.einsum("pj,bjxy->bpxy", edge_matrix(-1), below, precision=high_precision)
    high = jnp.einsum("pj,bjxy->bpxy", edge_matrix(1), above, precision=high_precision)
    pre_low = lax.slice_in_dim(pre, 0, HALO, axis=zaxis)
    pre_high = lax.slice_in_dim(pre, planes - HALO, planes, axis=zaxis)
    fresh_low = pre_low + courant[:HALO] * low
    fresh_high = pre_high + courant[planes - HALO :] * high
    return fresh_low, fresh_high


def on_device(
    forward_prev,
    forward_now,
    adjoint_prev,
    adjoint_now,
    courant,
    wavelet,
    sign_bits,
    source_depth,
    source_cell,
    receiver_depth,
    receiver_cell,
    residual_traces,
):
    planes, rows, cols = courant.shape
    lateral = rows * cols
    source_flat = source_depth * lateral + source_cell
    receiver_flat = receiver_depth * lateral + receiver_cell
    signs = (2 * sign_bits - 1).astype(jnp.float32)
    position = lax.axis_index("depth")
    zaxis = 1
    devices = lax.axis_size("depth")
    up = [(i, i + 1) for i in range(devices - 1)]
    down = [(i + 1, i) for i in range(devices - 1)]
    fields = [forward_now, adjoint_now]
    earlier = [forward_prev, adjoint_prev]
    send_up = jnp.concatenate([lax.slice_in_dim(f, planes - HALO, planes, axis=zaxis) for f in fields])
    send_down = jnp.concatenate([lax.slice_in_dim(f, 0, HALO, axis=zaxis) for f in fields])
    first_plane = position * planes
    correlation = None
    gate = ()
    for step in range(STEPS):
        below = lax.ppermute(send_up, "depth", up)
        above = lax.ppermute(send_down, "depth", down)
        if step > 0:
            gate, (source_flat, receiver_flat, signs, wavelet, residual_traces) = lax.optimization_barrier(
                (gate, (source_flat, receiver_flat, signs, wavelet, residual_traces))
            )
        terms = [
            spread(source_flat, signs * wavelet[step][None, :], first_plane, planes, rows, cols),
            spread(receiver_flat, residual_traces[:, step, :], first_plane, planes, rows, cols),
        ]
        pre = [local_part(fields[i], earlier[i], courant, terms[i], zaxis) for i in range(2)]
        pre = lax.optimization_barrier(pre)
        edges = [
            edge_parts(pre[i], below[i : i + 1], above[i : i + 1], courant, zaxis) for i in range(2)
        ]
        send_up = jnp.concatenate([edges[0][1], edges[1][1]])
        send_down = jnp.concatenate([edges[0][0], edges[1][0]])
        gate = (send_up, send_down)
        fresh = []
        for i in range(2):
            middle = lax.slice_in_dim(pre[i], HALO, planes - HALO, axis=zaxis)
            fresh.append(jnp.concatenate([edges[i][0], middle, edges[i][1]], axis=zaxis))
        part = fresh[0][0] * fresh[1][0]
        correlation = part if correlation is None else correlation + part
        earlier, fields = fields, fresh
    lateral_smooth = smooth(smooth(correlation, 1), 2)
    reduced = reduce_shots(lateral_smooth, 1)
    columns = lax.all_to_all(reduced, "depth", split_axis=1, concat_axis=0, tiled=True)
    gradient = smooth(columns, 0)
    return (earlier[0], fields[0], earlier[1], fields[1], gradient)


def solution(mesh):
    in_specs = (
        P("shots", "depth", None, None),
        P("shots", "depth", None, None),
        P("shots", "depth", None, None),
        P("shots", "depth", None, None),
        P("depth", None, None),
        P(),
        P("shots", None),
        P(),
        P(),
        P(),
        P(),
        P("shots", None, None),
    )
    out_specs = (
        P("shots", "depth", None, None),
        P("shots", "depth", None, None),
        P("shots", "depth", None, None),
        P("shots", "depth", None, None),
        P(None, ("shots", "depth"), None),
    )
    return jax.shard_map(
        on_device, mesh=mesh, in_specs=in_specs, out_specs=out_specs, check_vma=False
    )
```

```python
import jax
import jax.numpy as jnp
from jax import lax
from jax.sharding import PartitionSpec as P

STEPS = 2
HALO = 4


COEFFS = (-205.0 / 72.0, 8.0 / 5.0, -1.0 / 5.0, 8.0 / 315.0, -1.0 / 560.0)
KERNEL = (1.0 / 16.0, 4.0 / 16.0, 6.0 / 16.0, 4.0 / 16.0, 1.0 / 16.0)


def shifted(values, axis, offset):
    size = values.shape[axis]
    width = abs(offset)
    pads = [(0, 0, 0)] * values.ndim
    if offset > 0:
        kept = lax.slice_in_dim(values, offset, size, axis=axis)
        pads[axis] = (0, width, 0)
    else:
        kept = lax.slice_in_dim(values, 0, size - width, axis=axis)
        pads[axis] = (width, 0, 0)
    return lax.pad(kept, jnp.array(0.0, values.dtype), pads)


def band(size):
    index = jnp.arange(size)
    gap = jnp.abs(index[:, None] - index[None, :])
    matrix = jnp.zeros((size, size), jnp.float32)
    for k in range(1, 5):
        matrix = jnp.where(gap == k, jnp.float32(COEFFS[k]), matrix)
    return matrix


def lateral_laplace(core, zaxis):
    rows, cols = core.shape[zaxis + 1], core.shape[zaxis + 2]
    high = lax.Precision.HIGHEST
    along_y = jnp.einsum("...xy,yk->...xk", core, band(cols), precision=high)
    along_x = jnp.einsum("...xy,kx->...ky", core, band(rows), precision=high)
    return 3.0 * COEFFS[0] * core + (along_x + along_y)


def depth_laplace(below, core, above, zaxis):
    planes = core.shape[zaxis]
    extended = jnp.concatenate([below, core, above], axis=zaxis)
    total = None
    for k in range(1, 5):
        near = lax.slice_in_dim(extended, HALO + k, HALO + k + planes, axis=zaxis) + lax.slice_in_dim(
            extended, HALO - k, HALO - k + planes, axis=zaxis
        )
        total = COEFFS[k] * near if total is None else total + COEFFS[k] * near
    return total


def smooth(values, axis):
    total = KERNEL[2] * values
    for k in (1, 2):
        total = total + KERNEL[2 + k] * (shifted(values, axis, k) + shifted(values, axis, -k))
    return total


def exchange(current, dim):
    devices = lax.axis_size("depth")
    length = current.shape[dim]
    up = [(i, i + 1) for i in range(devices - 1)]
    down = [(i + 1, i) for i in range(devices - 1)]
    last = lax.slice_in_dim(current, length - HALO, length, axis=dim)
    leading = lax.slice_in_dim(current, 0, HALO, axis=dim)
    below = lax.ppermute(last, "depth", up)
    above = lax.ppermute(leading, "depth", down)
    return below, above


def spread(flat, values, first_plane, planes, rows, cols):
    lateral = rows * cols
    limit = planes * lateral
    local = flat - first_plane * lateral
    local = jnp.where((local >= 0) & (local < limit), local, limit)
    grid = jnp.zeros((values.shape[0], limit), jnp.float32).at[:, local].add(values, mode="drop")
    return grid.reshape(values.shape[0], planes, rows, cols)


def spread_dense(depth, cell, values, first_plane, planes, rows, cols):
    steps, count = values.shape
    local = depth - first_plane
    inside = (local >= 0) & (local < planes)
    row_id = jnp.where(inside, local * rows + cell // cols, -1)
    by_row = (row_id[None, :] == jnp.arange(planes * rows)[:, None]).astype(jnp.bfloat16)
    by_col = (cell % cols)[:, None] == jnp.arange(cols)[None, :]
    pieces = []
    rest = values
    for _ in range(3):
        piece = lax.reduce_precision(rest, exponent_bits=8, mantissa_bits=7)
        rest = rest - piece
        pieces.append(piece.astype(jnp.bfloat16))
    stacked = jnp.stack(pieces)
    right = jnp.where(by_col[None, None], stacked[:, :, :, None], jnp.zeros((), jnp.bfloat16))
    right = right.transpose(2, 0, 1, 3).reshape(count, 3 * steps * cols)
    grid = jnp.dot(by_row, right, preferred_element_type=jnp.float32)
    grid = grid.reshape(planes * rows, 3, steps, cols)
    grid = grid[:, 0] + grid[:, 1] + grid[:, 2]
    return grid.transpose(1, 0, 2).reshape(steps, planes, rows, cols)


def reduce_shots(values, dim):
    devices = lax.axis_size("shots")
    me = lax.axis_index("shots")
    length = values.shape[dim]
    shape = values.shape
    blocks = values.reshape(shape[:dim] + (devices, length // devices) + shape[dim + 1 :])
    bit = 1
    while bit < devices:
        count = blocks.shape[dim]
        paired = blocks.reshape(shape[:dim] + (count // 2, 2, length // devices) + shape[dim + 1 :])
        mine = (me // bit) % 2
        keep = lax.dynamic_index_in_dim(paired, mine, axis=dim + 1, keepdims=False)
        send = lax.dynamic_index_in_dim(paired, 1 - mine, axis=dim + 1, keepdims=False)
        pairs = [(i, i ^ bit) for i in range(devices)]
        blocks = keep + lax.ppermute(send, "shots", pairs)
        bit *= 2
    return blocks.reshape(shape[:dim] + (length // devices,) + shape[dim + 1 :])


def on_device(
    forward_prev,
    forward_now,
    adjoint_prev,
    adjoint_now,
    courant,
    wavelet,
    sign_bits,
    source_depth,
    source_cell,
    receiver_depth,
    receiver_cell,
    residual_traces,
):
    planes, rows, cols = courant.shape
    lateral = rows * cols
    source_flat = source_depth * lateral + source_cell
    receiver_flat = receiver_depth * lateral + receiver_cell
    signs = (2 * sign_bits - 1).astype(jnp.float32)
    position = lax.axis_index("depth")
    earlier = jnp.stack([forward_prev, adjoint_prev])
    current = jnp.stack([forward_now, adjoint_now])
    zaxis = 2
    below, above = exchange(current, zaxis)
    first_plane = position * planes
    correlation = None
    forward_terms = spread_dense(source_depth, source_cell, signs[0][None, :] * wavelet, first_plane, planes, rows, cols)
    adjoint_terms = spread_dense(receiver_depth, receiver_cell, residual_traces[0], first_plane, planes, rows, cols)
    for step in range(STEPS):
        terms = jnp.stack([forward_terms[step : step + 1], adjoint_terms[step : step + 1]])
        lateral_part = lateral_laplace(current, zaxis)
        fresh = (
            2.0 * current
            - earlier
            + courant * (lateral_part + depth_laplace(below, current, above, zaxis))
            + terms
        )
        if step + 1 < STEPS:
            below, above = exchange(fresh, zaxis)
        part = fresh[0, 0] * fresh[1, 0]
        correlation = part if correlation is None else correlation + part
        earlier, current = (current, fresh)
    lateral_smooth = smooth(smooth(correlation, 1), 2)
    reduced = reduce_shots(lateral_smooth, 1)
    columns = lax.all_to_all(reduced, "depth", split_axis=1, concat_axis=0, tiled=True)
    gradient = smooth(columns, 0)
    return (earlier[0], current[0], earlier[1], current[1], gradient)


def solution(mesh):
    in_specs = (
        P("shots", "depth", None, None),
        P("shots", "depth", None, None),
        P("shots", "depth", None, None),
        P("shots", "depth", None, None),
        P("depth", None, None),
        P(),
        P("shots", None),
        P(),
        P(),
        P(),
        P(),
        P("shots", None, None),
    )
    out_specs = (
        P("shots", "depth", None, None),
        P("shots", "depth", None, None),
        P("shots", "depth", None, None),
        P("shots", "depth", None, None),
        P(None, ("shots", "depth"), None),
    )
    return jax.shard_map(
        on_device, mesh=mesh, in_specs=in_specs, out_specs=out_specs, check_vma=False
    )
```

```python
import jax
import jax.numpy as jnp
from jax import lax
from jax.sharding import PartitionSpec as P

STEPS = 2
HALO = 4


COEFFS = (-205.0 / 72.0, 8.0 / 5.0, -1.0 / 5.0, 8.0 / 315.0, -1.0 / 560.0)
KERNEL = (1.0 / 16.0, 4.0 / 16.0, 6.0 / 16.0, 4.0 / 16.0, 1.0 / 16.0)


def shifted(values, axis, offset):
    size = values.shape[axis]
    width = abs(offset)
    pads = [(0, 0, 0)] * values.ndim
    if offset > 0:
        kept = lax.slice_in_dim(values, offset, size, axis=axis)
        pads[axis] = (0, width, 0)
    else:
        kept = lax.slice_in_dim(values, 0, size - width, axis=axis)
        pads[axis] = (width, 0, 0)
    return lax.pad(kept, jnp.array(0.0, values.dtype), pads)


def band(size):
    index = jnp.arange(size)
    gap = jnp.abs(index[:, None] - index[None, :])
    matrix = jnp.zeros((size, size), jnp.float32)
    for k in range(1, 5):
        matrix = jnp.where(gap == k, jnp.float32(COEFFS[k]), matrix)
    return matrix


def lateral_laplace(core, zaxis):
    rows, cols = core.shape[zaxis + 1], core.shape[zaxis + 2]
    high = lax.Precision.HIGHEST
    along_y = jnp.einsum("...xy,yk->...xk", core, band(cols), precision=high)
    along_x = jnp.einsum("...xy,kx->...ky", core, band(rows), precision=high)
    return 3.0 * COEFFS[0] * core + (along_x + along_y)


def depth_laplace(below, core, above, zaxis):
    planes = core.shape[zaxis]
    extended = jnp.concatenate([below, core, above], axis=zaxis)
    total = None
    for k in range(1, 5):
        near = lax.slice_in_dim(extended, HALO + k, HALO + k + planes, axis=zaxis) + lax.slice_in_dim(
            extended, HALO - k, HALO - k + planes, axis=zaxis
        )
        total = COEFFS[k] * near if total is None else total + COEFFS[k] * near
    return total


def smooth(values, axis):
    total = KERNEL[2] * values
    for k in (1, 2):
        total = total + KERNEL[2 + k] * (shifted(values, axis, k) + shifted(values, axis, -k))
    return total


def exchange(current, dim):
    devices = lax.axis_size("depth")
    length = current.shape[dim]
    up = [(i, i + 1) for i in range(devices - 1)]
    down = [(i + 1, i) for i in range(devices - 1)]
    last = lax.slice_in_dim(current, length - HALO, length, axis=dim)
    leading = lax.slice_in_dim(current, 0, HALO, axis=dim)
    below = lax.ppermute(last, "depth", up)
    above = lax.ppermute(leading, "depth", down)
    return below, above


def spread(flat, values, first_plane, planes, rows, cols):
    lateral = rows * cols
    limit = planes * lateral
    local = flat - first_plane * lateral
    local = jnp.where((local >= 0) & (local < limit), local, limit)
    grid = jnp.zeros((values.shape[0], limit), jnp.float32).at[:, local].add(values, mode="drop")
    return grid.reshape(values.shape[0], planes, rows, cols)


def spread_dense(depth, cell, values, first_plane, planes, rows, cols):
    steps, count = values.shape
    local = depth - first_plane
    inside = (local >= 0) & (local < planes)
    row_id = jnp.where(inside, local * rows + cell // cols, -1)
    by_row = (row_id[None, :] == jnp.arange(planes * rows)[:, None]).astype(jnp.bfloat16)
    by_col = (cell % cols)[:, None] == jnp.arange(cols)[None, :]
    pieces = []
    rest = values
    for _ in range(3):
        piece = lax.reduce_precision(rest, exponent_bits=8, mantissa_bits=7)
        rest = rest - piece
        pieces.append(piece.astype(jnp.bfloat16))
    stacked = jnp.stack(pieces)
    right = jnp.where(by_col[None, None], stacked[:, :, :, None], jnp.zeros((), jnp.bfloat16))
    right = right.transpose(2, 0, 1, 3).reshape(count, 3 * steps * cols)
    grid = jnp.dot(by_row, right, preferred_element_type=jnp.float32)
    grid = grid.reshape(planes * rows, 3, steps, cols)
    grid = grid[:, 0] + grid[:, 1] + grid[:, 2]
    return grid.transpose(1, 0, 2).reshape(steps, planes, rows, cols)


def reduce_shots(values, dim):
    devices = lax.axis_size("shots")
    me = lax.axis_index("shots")
    length = values.shape[dim]
    shape = values.shape
    blocks = values.reshape(shape[:dim] + (devices, length // devices) + shape[dim + 1 :])
    bit = 1
    while bit < devices:
        count = blocks.shape[dim]
        paired = blocks.reshape(shape[:dim] + (count // 2, 2, length // devices) + shape[dim + 1 :])
        mine = (me // bit) % 2
        keep = lax.dynamic_index_in_dim(paired, mine, axis=dim + 1, keepdims=False)
        send = lax.dynamic_index_in_dim(paired, 1 - mine, axis=dim + 1, keepdims=False)
        pairs = [(i, i ^ bit) for i in range(devices)]
        blocks = keep + lax.ppermute(send, "shots", pairs)
        bit *= 2
    return blocks.reshape(shape[:dim] + (length // devices,) + shape[dim + 1 :])


def halves(current, earlier, courant, terms, zaxis):
    planes = current.shape[zaxis]
    lateral = lateral_laplace(current, zaxis)
    low = lambda a, lo=0: lax.slice_in_dim(a, lo, lo + HALO, axis=a.ndim - 3)
    parts = []
    for first, sign in ((0, 1), (planes - HALO, -1)):
        inner = None
        for k in range(1, 5):
            piece = COEFFS[k] * low(current, first + sign * k)
            inner = piece if inner is None else inner + piece
        update = (
            2.0 * low(current, first)
            - low(earlier, first)
            + low(courant, first) * (low(lateral, first) + inner)
            + low(terms, first)
        )
        parts.append(update)
    return parts


def finish_low(partial, current, below, courant, zaxis):
    extended = jnp.concatenate([below, lax.slice_in_dim(current, 0, HALO, axis=zaxis)], axis=zaxis)
    outer = None
    for k in range(1, 5):
        piece = COEFFS[k] * lax.slice_in_dim(extended, HALO - k, 2 * HALO - k, axis=zaxis)
        outer = piece if outer is None else outer + piece
    return partial + courant[:HALO] * outer


def finish_high(partial, current, above, courant, zaxis):
    planes = current.shape[zaxis]
    extended = jnp.concatenate([lax.slice_in_dim(current, planes - HALO, planes, axis=zaxis), above], axis=zaxis)
    outer = None
    for k in range(1, 5):
        piece = COEFFS[k] * lax.slice_in_dim(extended, k, k + HALO, axis=zaxis)
        outer = piece if outer is None else outer + piece
    return partial + courant[planes - HALO :] * outer


def gradient_part(correlation):
    reduced = reduce_shots(smooth(smooth(correlation, 1), 2), 1)
    return lax.all_to_all(reduced, "depth", split_axis=1, concat_axis=0, tiled=True)


def on_device(
    forward_prev,
    forward_now,
    adjoint_prev,
    adjoint_now,
    courant,
    wavelet,
    sign_bits,
    source_depth,
    source_cell,
    receiver_depth,
    receiver_cell,
    residual_traces,
):
    planes, rows, cols = courant.shape
    assert planes == 2 * HALO and STEPS == 2
    signs = (2 * sign_bits - 1).astype(jnp.float32)
    position = lax.axis_index("depth")
    devices = lax.axis_size("depth")
    up = [(i, i + 1) for i in range(devices - 1)]
    down = [(i + 1, i) for i in range(devices - 1)]
    earlier = jnp.stack([forward_prev, adjoint_prev])
    current = jnp.stack([forward_now, adjoint_now])
    zaxis = 2
    first_plane = position * planes
    forward_terms = spread_dense(source_depth, source_cell, signs[0][None, :] * wavelet, first_plane, planes, rows, cols)
    adjoint_terms = spread_dense(receiver_depth, receiver_cell, residual_traces[0], first_plane, planes, rows, cols)
    terms = [jnp.stack([forward_terms[t : t + 1], adjoint_terms[t : t + 1]]) for t in range(STEPS)]

    below = lax.ppermute(lax.slice_in_dim(current, HALO, planes, axis=zaxis), "depth", up)
    above = lax.ppermute(lax.slice_in_dim(current, 0, HALO, axis=zaxis), "depth", down)
    part_low, part_high = lax.optimization_barrier(halves(current, earlier, courant, terms[0], zaxis))
    first_low = finish_low(part_low, current, below, courant, zaxis)
    next_above = lax.ppermute(first_low, "depth", down)
    first_high = finish_high(part_high, current, above, courant, zaxis)
    next_below = lax.ppermute(first_high, "depth", up)
    first = jnp.concatenate([first_low, first_high], axis=zaxis)

    part_low, part_high = lax.optimization_barrier(halves(first, current, courant, terms[1], zaxis))
    second_high = finish_high(part_high, first, next_above, courant, zaxis)
    high = gradient_part(first_high[0, 0] * first_high[1, 0] + second_high[0, 0] * second_high[1, 0])
    second_low = finish_low(part_low, first, next_below, courant, zaxis)
    second = jnp.concatenate([second_low, second_high], axis=zaxis)

    low = gradient_part(first_low[0, 0] * first_low[1, 0] + second_low[0, 0] * second_low[1, 0])
    width = low.shape[1]
    columns = jnp.stack(
        [low.reshape(devices, HALO, width, cols), high.reshape(devices, HALO, width, cols)], axis=1
    ).reshape(devices * planes, width, cols)
    gradient = smooth(columns, 0)
    return (first[0], second[0], first[1], second[1], gradient)


def solution(mesh):
    in_specs = (
        P("shots", "depth", None, None),
        P("shots", "depth", None, None),
        P("shots", "depth", None, None),
        P("shots", "depth", None, None),
        P("depth", None, None),
        P(),
        P("shots", None),
        P(),
        P(),
        P(),
        P(),
        P("shots", None, None),
    )
    out_specs = (
        P("shots", "depth", None, None),
        P("shots", "depth", None, None),
        P("shots", "depth", None, None),
        P("shots", "depth", None, None),
        P(None, ("shots", "depth"), None),
    )
    return jax.shard_map(
        on_device, mesh=mesh, in_specs=in_specs, out_specs=out_specs, check_vma=False
    )
```

```python
import jax
import jax.numpy as jnp
from jax import lax
from jax.sharding import PartitionSpec as P

STEPS = 2
HALO = 4


COEFFS = (-205.0 / 72.0, 8.0 / 5.0, -1.0 / 5.0, 8.0 / 315.0, -1.0 / 560.0)
KERNEL = (1.0 / 16.0, 4.0 / 16.0, 6.0 / 16.0, 4.0 / 16.0, 1.0 / 16.0)


def shifted(values, axis, offset):
    size = values.shape[axis]
    width = abs(offset)
    pads = [(0, 0, 0)] * values.ndim
    if offset > 0:
        kept = lax.slice_in_dim(values, offset, size, axis=axis)
        pads[axis] = (0, width, 0)
    else:
        kept = lax.slice_in_dim(values, 0, size - width, axis=axis)
        pads[axis] = (width, 0, 0)
    return lax.pad(kept, jnp.array(0.0, values.dtype), pads)


def band(size):
    index = jnp.arange(size)
    gap = jnp.abs(index[:, None] - index[None, :])
    matrix = jnp.zeros((size, size), jnp.float32)
    for k in range(1, 5):
        matrix = jnp.where(gap == k, jnp.float32(COEFFS[k]), matrix)
    return matrix


def lateral_laplace(core, zaxis):
    rows, cols = core.shape[zaxis + 1], core.shape[zaxis + 2]
    high = lax.Precision.HIGHEST
    along_y = jnp.einsum("...xy,yk->...xk", core, band(cols), precision=high)
    along_x = jnp.einsum("...xy,kx->...ky", core, band(rows), precision=high)
    return 3.0 * COEFFS[0] * core + (along_x + along_y)


def depth_laplace(below, core, above, zaxis):
    planes = core.shape[zaxis]
    extended = jnp.concatenate([below, core, above], axis=zaxis)
    total = None
    for k in range(1, 5):
        near = lax.slice_in_dim(extended, HALO + k, HALO + k + planes, axis=zaxis) + lax.slice_in_dim(
            extended, HALO - k, HALO - k + planes, axis=zaxis
        )
        total = COEFFS[k] * near if total is None else total + COEFFS[k] * near
    return total


def smooth(values, axis):
    total = KERNEL[2] * values
    for k in (1, 2):
        total = total + KERNEL[2 + k] * (shifted(values, axis, k) + shifted(values, axis, -k))
    return total


def exchange(current, dim):
    devices = lax.axis_size("depth")
    length = current.shape[dim]
    up = [(i, i + 1) for i in range(devices - 1)]
    down = [(i + 1, i) for i in range(devices - 1)]
    last = lax.slice_in_dim(current, length - HALO, length, axis=dim)
    leading = lax.slice_in_dim(current, 0, HALO, axis=dim)
    below = lax.ppermute(last, "depth", up)
    above = lax.ppermute(leading, "depth", down)
    return below, above


def spread(flat, values, first_plane, planes, rows, cols):
    lateral = rows * cols
    limit = planes * lateral
    local = flat - first_plane * lateral
    local = jnp.where((local >= 0) & (local < limit), local, limit)
    grid = jnp.zeros((values.shape[0], limit), jnp.float32).at[:, local].add(values, mode="drop")
    return grid.reshape(values.shape[0], planes, rows, cols)


def spread_dense(depth, cell, values, first_plane, planes, rows, cols):
    steps, count = values.shape
    local = depth - first_plane
    inside = (local >= 0) & (local < planes)
    row_id = jnp.where(inside, local * rows + cell // cols, -1)
    by_row = (row_id[None, :] == jnp.arange(planes * rows)[:, None]).astype(jnp.bfloat16)
    by_col = (cell % cols)[:, None] == jnp.arange(cols)[None, :]
    pieces = []
    rest = values
    for _ in range(3):
        piece = lax.reduce_precision(rest, exponent_bits=8, mantissa_bits=7)
        rest = rest - piece
        pieces.append(piece.astype(jnp.bfloat16))
    stacked = jnp.stack(pieces)
    right = jnp.where(by_col[None, None], stacked[:, :, :, None], jnp.zeros((), jnp.bfloat16))
    right = right.transpose(2, 0, 1, 3).reshape(count, 3 * steps * cols)
    grid = jnp.dot(by_row, right, preferred_element_type=jnp.float32)
    grid = grid.reshape(planes * rows, 3, steps, cols)
    grid = grid[:, 0] + grid[:, 1] + grid[:, 2]
    return grid.transpose(1, 0, 2).reshape(steps, planes, rows, cols)


def reduce_shots(values, dim):
    devices = lax.axis_size("shots")
    me = lax.axis_index("shots")
    length = values.shape[dim]
    shape = values.shape
    blocks = values.reshape(shape[:dim] + (devices, length // devices) + shape[dim + 1 :])
    bit = 1
    while bit < devices:
        count = blocks.shape[dim]
        paired = blocks.reshape(shape[:dim] + (count // 2, 2, length // devices) + shape[dim + 1 :])
        mine = (me // bit) % 2
        keep = lax.dynamic_index_in_dim(paired, mine, axis=dim + 1, keepdims=False)
        send = lax.dynamic_index_in_dim(paired, 1 - mine, axis=dim + 1, keepdims=False)
        pairs = [(i, i ^ bit) for i in range(devices)]
        blocks = keep + lax.ppermute(send, "shots", pairs)
        bit *= 2
    return blocks.reshape(shape[:dim] + (length // devices,) + shape[dim + 1 :])


def on_device(
    forward_prev,
    forward_now,
    adjoint_prev,
    adjoint_now,
    courant,
    wavelet,
    sign_bits,
    source_depth,
    source_cell,
    receiver_depth,
    receiver_cell,
    residual_traces,
):
    planes, rows, cols = courant.shape
    lateral = rows * cols
    source_flat = source_depth * lateral + source_cell
    receiver_flat = receiver_depth * lateral + receiver_cell
    signs = (2 * sign_bits - 1).astype(jnp.float32)
    position = lax.axis_index("depth")
    earlier = jnp.stack([forward_prev, adjoint_prev])
    current = jnp.stack([forward_now, adjoint_now])
    zaxis = 2
    below, above = exchange(current, zaxis)
    first_plane = position * planes
    correlation = None
    forward_terms = spread_dense(source_depth, source_cell, signs[0][None, :] * wavelet, first_plane, planes, rows, cols)
    adjoint_terms = spread_dense(receiver_depth, receiver_cell, residual_traces[0], first_plane, planes, rows, cols)
    for step in range(STEPS):
        terms = jnp.stack([forward_terms[step : step + 1], adjoint_terms[step : step + 1]])
        partial = lax.optimization_barrier(
            2.0 * current - earlier + courant * lateral_laplace(current, zaxis) + terms
        )
        fresh = partial + courant * depth_laplace(below, current, above, zaxis)
        if step + 1 < STEPS:
            below, above = exchange(fresh, zaxis)
        part = fresh[0, 0] * fresh[1, 0]
        correlation = part if correlation is None else correlation + part
        earlier, current = (current, fresh)
    lateral_smooth = smooth(smooth(correlation, 1), 2)
    reduced = reduce_shots(lateral_smooth, 1)
    columns = lax.all_to_all(reduced, "depth", split_axis=1, concat_axis=0, tiled=True)
    gradient = smooth(columns, 0)
    return (earlier[0], current[0], earlier[1], current[1], gradient)


def solution(mesh):
    in_specs = (
        P("shots", "depth", None, None),
        P("shots", "depth", None, None),
        P("shots", "depth", None, None),
        P("shots", "depth", None, None),
        P("depth", None, None),
        P(),
        P("shots", None),
        P(),
        P(),
        P(),
        P(),
        P("shots", None, None),
    )
    out_specs = (
        P("shots", "depth", None, None),
        P("shots", "depth", None, None),
        P("shots", "depth", None, None),
        P("shots", "depth", None, None),
        P(None, ("shots", "depth"), None),
    )
    return jax.shard_map(
        on_device, mesh=mesh, in_specs=in_specs, out_specs=out_specs, check_vma=False
    )
```

```python
import jax
import jax.numpy as jnp
from jax import lax
from jax.sharding import PartitionSpec as P

STEPS = 2
HALO = 4


COEFFS = (-205.0 / 72.0, 8.0 / 5.0, -1.0 / 5.0, 8.0 / 315.0, -1.0 / 560.0)
KERNEL = (1.0 / 16.0, 4.0 / 16.0, 6.0 / 16.0, 4.0 / 16.0, 1.0 / 16.0)


def shifted(values, axis, offset):
    size = values.shape[axis]
    width = abs(offset)
    pads = [(0, 0, 0)] * values.ndim
    if offset > 0:
        kept = lax.slice_in_dim(values, offset, size, axis=axis)
        pads[axis] = (0, width, 0)
    else:
        kept = lax.slice_in_dim(values, 0, size - width, axis=axis)
        pads[axis] = (width, 0, 0)
    return lax.pad(kept, jnp.array(0.0, values.dtype), pads)


def band(size):
    index = jnp.arange(size)
    gap = jnp.abs(index[:, None] - index[None, :])
    matrix = jnp.zeros((size, size), jnp.float32)
    for k in range(1, 5):
        matrix = jnp.where(gap == k, jnp.float32(COEFFS[k]), matrix)
    return matrix


def lateral_laplace(core, zaxis):
    rows, cols = core.shape[zaxis + 1], core.shape[zaxis + 2]
    high = lax.Precision.HIGHEST
    along_y = jnp.einsum("...xy,yk->...xk", core, band(cols), precision=high)
    along_x = jnp.einsum("...xy,kx->...ky", core, band(rows), precision=high)
    return 3.0 * COEFFS[0] * core + (along_x + along_y)


def depth_laplace(below, core, above, zaxis):
    planes = core.shape[zaxis]
    extended = jnp.concatenate([below, core, above], axis=zaxis)
    total = None
    for k in range(1, 5):
        near = lax.slice_in_dim(extended, HALO + k, HALO + k + planes, axis=zaxis) + lax.slice_in_dim(
            extended, HALO - k, HALO - k + planes, axis=zaxis
        )
        total = COEFFS[k] * near if total is None else total + COEFFS[k] * near
    return total


def smooth(values, axis):
    total = KERNEL[2] * values
    for k in (1, 2):
        total = total + KERNEL[2 + k] * (shifted(values, axis, k) + shifted(values, axis, -k))
    return total


def exchange(fields, dim):
    devices = lax.axis_size("depth")
    length = fields[0].shape[dim]
    up = [(i, i + 1) for i in range(devices - 1)]
    down = [(i + 1, i) for i in range(devices - 1)]
    last = tuple(lax.slice_in_dim(f, length - HALO, length, axis=dim) for f in fields)
    leading = tuple(lax.slice_in_dim(f, 0, HALO, axis=dim) for f in fields)
    below = lax.ppermute(last, "depth", up)
    above = lax.ppermute(leading, "depth", down)
    return below, above


def spread(flat, values, first_plane, planes, rows, cols):
    lateral = rows * cols
    limit = planes * lateral
    local = flat - first_plane * lateral
    local = jnp.where((local >= 0) & (local < limit), local, limit)
    grid = jnp.zeros((values.shape[0], limit), jnp.float32).at[:, local].add(values, mode="drop")
    return grid.reshape(values.shape[0], planes, rows, cols)


def spread_dense(depth, cell, values, first_plane, planes, rows, cols):
    steps, count = values.shape
    local = depth - first_plane
    inside = (local >= 0) & (local < planes)
    row_id = jnp.where(inside, local * rows + cell // cols, -1)
    by_row = (row_id[None, :] == jnp.arange(planes * rows)[:, None]).astype(jnp.bfloat16)
    by_col = (cell % cols)[:, None] == jnp.arange(cols)[None, :]
    pieces = []
    rest = values
    for _ in range(3):
        piece = lax.reduce_precision(rest, exponent_bits=8, mantissa_bits=7)
        rest = rest - piece
        pieces.append(piece.astype(jnp.bfloat16))
    stacked = jnp.stack(pieces)
    right = jnp.where(by_col[None, None], stacked[:, :, :, None], jnp.zeros((), jnp.bfloat16))
    right = right.transpose(2, 0, 1, 3).reshape(count, 3 * steps * cols)
    grid = jnp.dot(by_row, right, preferred_element_type=jnp.float32)
    grid = grid.reshape(planes * rows, 3, steps, cols)
    grid = grid[:, 0] + grid[:, 1] + grid[:, 2]
    return grid.transpose(1, 0, 2).reshape(steps, planes, rows, cols)


def reduce_shots(values, dim):
    devices = lax.axis_size("shots")
    me = lax.axis_index("shots")
    length = values.shape[dim]
    shape = values.shape
    blocks = values.reshape(shape[:dim] + (devices, length // devices) + shape[dim + 1 :])
    bit = 1
    while bit < devices:
        count = blocks.shape[dim]
        paired = blocks.reshape(shape[:dim] + (count // 2, 2, length // devices) + shape[dim + 1 :])
        mine = (me // bit) % 2
        keep = lax.dynamic_index_in_dim(paired, mine, axis=dim + 1, keepdims=False)
        send = lax.dynamic_index_in_dim(paired, 1 - mine, axis=dim + 1, keepdims=False)
        pairs = [(i, i ^ bit) for i in range(devices)]
        blocks = keep + lax.ppermute(send, "shots", pairs)
        bit *= 2
    return blocks.reshape(shape[:dim] + (length // devices,) + shape[dim + 1 :])


def on_device(
    forward_prev,
    forward_now,
    adjoint_prev,
    adjoint_now,
    courant,
    wavelet,
    sign_bits,
    source_depth,
    source_cell,
    receiver_depth,
    receiver_cell,
    residual_traces,
):
    planes, rows, cols = courant.shape
    lateral = rows * cols
    source_flat = source_depth * lateral + source_cell
    receiver_flat = receiver_depth * lateral + receiver_cell
    signs = (2 * sign_bits - 1).astype(jnp.float32)
    position = lax.axis_index("depth")
    earlier = [forward_prev, adjoint_prev]
    current = [forward_now, adjoint_now]
    zaxis = 1
    below, above = exchange(current, zaxis)
    first_plane = position * planes
    correlation = None
    forward_terms = spread_dense(source_depth, source_cell, signs[0][None, :] * wavelet, first_plane, planes, rows, cols)
    adjoint_terms = spread_dense(receiver_depth, receiver_cell, residual_traces[0], first_plane, planes, rows, cols)
    for step in range(STEPS):
        terms = [forward_terms[step : step + 1], adjoint_terms[step : step + 1]]
        partial = lax.optimization_barrier(
            [
                2.0 * current[i] - earlier[i] + courant * lateral_laplace(current[i], zaxis) + terms[i]
                for i in range(2)
            ]
        )
        fresh = [
            partial[i] + courant * depth_laplace(below[i], current[i], above[i], zaxis) for i in range(2)
        ]
        if step + 1 < STEPS:
            below, above = exchange(fresh, zaxis)
        part = fresh[0][0] * fresh[1][0]
        correlation = part if correlation is None else correlation + part
        earlier, current = (current, fresh)
    lateral_smooth = smooth(smooth(correlation, 1), 2)
    reduced = reduce_shots(lateral_smooth, 1)
    columns = lax.all_to_all(reduced, "depth", split_axis=1, concat_axis=0, tiled=True)
    gradient = smooth(columns, 0)
    return (earlier[0], current[0], earlier[1], current[1], gradient)


def solution(mesh):
    in_specs = (
        P("shots", "depth", None, None),
        P("shots", "depth", None, None),
        P("shots", "depth", None, None),
        P("shots", "depth", None, None),
        P("depth", None, None),
        P(),
        P("shots", None),
        P(),
        P(),
        P(),
        P(),
        P("shots", None, None),
    )
    out_specs = (
        P("shots", "depth", None, None),
        P("shots", "depth", None, None),
        P("shots", "depth", None, None),
        P("shots", "depth", None, None),
        P(None, ("shots", "depth"), None),
    )
    return jax.shard_map(
        on_device, mesh=mesh, in_specs=in_specs, out_specs=out_specs, check_vma=False
    )
```

```python
import jax
import jax.numpy as jnp
from jax import lax
from jax.sharding import PartitionSpec as P

STEPS = 2
HALO = 4


COEFFS = (-205.0 / 72.0, 8.0 / 5.0, -1.0 / 5.0, 8.0 / 315.0, -1.0 / 560.0)
KERNEL = (1.0 / 16.0, 4.0 / 16.0, 6.0 / 16.0, 4.0 / 16.0, 1.0 / 16.0)


def shifted(values, axis, offset):
    size = values.shape[axis]
    width = abs(offset)
    pads = [(0, 0, 0)] * values.ndim
    if offset > 0:
        kept = lax.slice_in_dim(values, offset, size, axis=axis)
        pads[axis] = (0, width, 0)
    else:
        kept = lax.slice_in_dim(values, 0, size - width, axis=axis)
        pads[axis] = (width, 0, 0)
    return lax.pad(kept, jnp.array(0.0, values.dtype), pads)


def band(size):
    index = jnp.arange(size)
    gap = jnp.abs(index[:, None] - index[None, :])
    matrix = jnp.zeros((size, size), jnp.float32)
    for k in range(1, 5):
        matrix = jnp.where(gap == k, jnp.float32(COEFFS[k]), matrix)
    return matrix


def lateral_laplace(core, zaxis):
    rows, cols = core.shape[zaxis + 1], core.shape[zaxis + 2]
    high = lax.Precision.HIGHEST
    along_y = jnp.einsum("...xy,yk->...xk", core, band(cols), precision=high)
    along_x = jnp.einsum("...xy,kx->...ky", core, band(rows), precision=high)
    return 3.0 * COEFFS[0] * core + (along_x + along_y)


def depth_laplace(below, core, above, zaxis):
    planes = core.shape[zaxis]
    extended = jnp.concatenate([below, core, above], axis=zaxis)
    total = None
    for k in range(1, 5):
        near = lax.slice_in_dim(extended, HALO + k, HALO + k + planes, axis=zaxis) + lax.slice_in_dim(
            extended, HALO - k, HALO - k + planes, axis=zaxis
        )
        total = COEFFS[k] * near if total is None else total + COEFFS[k] * near
    return total


def smooth(values, axis):
    total = KERNEL[2] * values
    for k in (1, 2):
        total = total + KERNEL[2 + k] * (shifted(values, axis, k) + shifted(values, axis, -k))
    return total


def exchange(fields, dim):
    devices = lax.axis_size("depth")
    length = fields[0].shape[dim]
    up = [(i, i + 1) for i in range(devices - 1)]
    down = [(i + 1, i) for i in range(devices - 1)]
    last = tuple(lax.slice_in_dim(f, length - HALO, length, axis=dim) for f in fields)
    leading = tuple(lax.slice_in_dim(f, 0, HALO, axis=dim) for f in fields)
    below = lax.ppermute(last, "depth", up)
    above = lax.ppermute(leading, "depth", down)
    return below, above


def spread(flat, values, first_plane, planes, rows, cols):
    lateral = rows * cols
    limit = planes * lateral
    local = flat - first_plane * lateral
    local = jnp.where((local >= 0) & (local < limit), local, limit)
    grid = jnp.zeros((values.shape[0], limit), jnp.float32).at[:, local].add(values, mode="drop")
    return grid.reshape(values.shape[0], planes, rows, cols)


def spread_dense(depth, cell, values, first_plane, planes, rows, cols):
    steps, count = values.shape
    local = depth - first_plane
    inside = (local >= 0) & (local < planes)
    row_id = jnp.where(inside, local * rows + cell // cols, -1)
    by_row = (row_id[None, :] == jnp.arange(planes * rows)[:, None]).astype(jnp.bfloat16)
    by_col = (cell % cols)[:, None] == jnp.arange(cols)[None, :]
    pieces = []
    rest = values
    for _ in range(3):
        piece = lax.reduce_precision(rest, exponent_bits=8, mantissa_bits=7)
        rest = rest - piece
        pieces.append(piece.astype(jnp.bfloat16))
    stacked = jnp.stack(pieces)
    right = jnp.where(by_col[None, None], stacked[:, :, :, None], jnp.zeros((), jnp.bfloat16))
    right = right.transpose(2, 0, 1, 3).reshape(count, 3 * steps * cols)
    grid = jnp.dot(by_row, right, preferred_element_type=jnp.float32)
    grid = grid.reshape(planes * rows, 3, steps, cols)
    grid = grid[:, 0] + grid[:, 1] + grid[:, 2]
    return grid.transpose(1, 0, 2).reshape(steps, planes, rows, cols)


def reduce_shots(values, dim):
    devices = lax.axis_size("shots")
    me = lax.axis_index("shots")
    length = values.shape[dim]
    shape = values.shape
    blocks = values.reshape(shape[:dim] + (devices, length // devices) + shape[dim + 1 :])
    bit = 1
    while bit < devices:
        count = blocks.shape[dim]
        paired = blocks.reshape(shape[:dim] + (count // 2, 2, length // devices) + shape[dim + 1 :])
        mine = (me // bit) % 2
        keep = lax.dynamic_index_in_dim(paired, mine, axis=dim + 1, keepdims=False)
        send = lax.dynamic_index_in_dim(paired, 1 - mine, axis=dim + 1, keepdims=False)
        pairs = [(i, i ^ bit) for i in range(devices)]
        blocks = keep + lax.ppermute(send, "shots", pairs)
        bit *= 2
    return blocks.reshape(shape[:dim] + (length // devices,) + shape[dim + 1 :])


def on_device(
    forward_prev,
    forward_now,
    adjoint_prev,
    adjoint_now,
    courant,
    wavelet,
    sign_bits,
    source_depth,
    source_cell,
    receiver_depth,
    receiver_cell,
    residual_traces,
):
    planes, rows, cols = courant.shape
    lateral = rows * cols
    source_flat = source_depth * lateral + source_cell
    receiver_flat = receiver_depth * lateral + receiver_cell
    signs = (2 * sign_bits - 1).astype(jnp.float32)
    position = lax.axis_index("depth")
    earlier = [forward_prev, adjoint_prev]
    current = [forward_now, adjoint_now]
    zaxis = 1
    below, above = exchange(current, zaxis)
    first_plane = position * planes
    correlation = None
    forward_terms = spread_dense(source_depth, source_cell, signs[0][None, :] * wavelet, first_plane, planes, rows, cols)
    adjoint_terms = spread_dense(receiver_depth, receiver_cell, residual_traces[0], first_plane, planes, rows, cols)
    for step in range(STEPS):
        terms = [forward_terms[step : step + 1], adjoint_terms[step : step + 1]]
        partial = lax.optimization_barrier(
            [
                2.0 * current[i] - earlier[i] + courant * lateral_laplace(current[i], zaxis) + terms[i]
                for i in range(2)
            ]
        )
        fresh = [
            partial[i] + courant * depth_laplace(below[i], current[i], above[i], zaxis) for i in range(2)
        ]
        if step + 1 < STEPS:
            below, above = exchange(fresh, zaxis)
        part = fresh[0][0] * fresh[1][0]
        correlation = part if correlation is None else correlation + part
        earlier, current = (current, fresh)
    lateral_smooth = smooth(smooth(correlation, 1), 2)
    moved = lax.all_to_all(lateral_smooth, ("shots", "depth"), split_axis=1, concat_axis=0, tiled=True)
    groups = lax.axis_size("shots")
    moved = moved.reshape((groups, moved.shape[0] // groups) + moved.shape[1:])
    columns = moved[0]
    for g in range(1, groups):
        columns = columns + moved[g]
    gradient = smooth(columns, 0)
    return (earlier[0], current[0], earlier[1], current[1], gradient)


def solution(mesh):
    in_specs = (
        P("shots", "depth", None, None),
        P("shots", "depth", None, None),
        P("shots", "depth", None, None),
        P("shots", "depth", None, None),
        P("depth", None, None),
        P(),
        P("shots", None),
        P(),
        P(),
        P(),
        P(),
        P("shots", None, None),
    )
    out_specs = (
        P("shots", "depth", None, None),
        P("shots", "depth", None, None),
        P("shots", "depth", None, None),
        P("shots", "depth", None, None),
        P(None, ("shots", "depth"), None),
    )
    return jax.shard_map(
        on_device, mesh=mesh, in_specs=in_specs, out_specs=out_specs, check_vma=False
    )
```

```python
import jax
import jax.numpy as jnp
from jax import lax
from jax.sharding import PartitionSpec as P

STEPS = 2
HALO = 4


COEFFS = (-205.0 / 72.0, 8.0 / 5.0, -1.0 / 5.0, 8.0 / 315.0, -1.0 / 560.0)
KERNEL = (1.0 / 16.0, 4.0 / 16.0, 6.0 / 16.0, 4.0 / 16.0, 1.0 / 16.0)


def shifted(values, axis, offset):
    size = values.shape[axis]
    width = abs(offset)
    pads = [(0, 0, 0)] * values.ndim
    if offset > 0:
        kept = lax.slice_in_dim(values, offset, size, axis=axis)
        pads[axis] = (0, width, 0)
    else:
        kept = lax.slice_in_dim(values, 0, size - width, axis=axis)
        pads[axis] = (width, 0, 0)
    return lax.pad(kept, jnp.array(0.0, values.dtype), pads)


def band(size):
    index = jnp.arange(size)
    gap = jnp.abs(index[:, None] - index[None, :])
    matrix = jnp.zeros((size, size), jnp.float32)
    for k in range(1, 5):
        matrix = jnp.where(gap == k, jnp.float32(COEFFS[k]), matrix)
    return matrix


def lateral_laplace(core, zaxis):
    rows, cols = core.shape[zaxis + 1], core.shape[zaxis + 2]
    high = lax.Precision.HIGHEST
    along_y = jnp.einsum("...xy,yk->...xk", core, band(cols), precision=high)
    along_x = jnp.einsum("...xy,kx->...ky", core, band(rows), precision=high)
    return 3.0 * COEFFS[0] * core + (along_x + along_y)


def depth_laplace(below, core, above, zaxis):
    planes = core.shape[zaxis]
    extended = jnp.concatenate([below, core, above], axis=zaxis)
    total = None
    for k in range(1, 5):
        near = lax.slice_in_dim(extended, HALO + k, HALO + k + planes, axis=zaxis) + lax.slice_in_dim(
            extended, HALO - k, HALO - k + planes, axis=zaxis
        )
        total = COEFFS[k] * near if total is None else total + COEFFS[k] * near
    return total


def smooth_matrix(size):
    index = jnp.arange(size)
    gap = index[:, None] - index[None, :]
    matrix = jnp.zeros((size, size), jnp.float32)
    for k in range(-2, 3):
        matrix = jnp.where(gap == k, jnp.float32(KERNEL[2 + k]), matrix)
    return matrix


def smooth_lateral(values):
    high = lax.Precision.HIGHEST
    rows, cols = values.shape[-2], values.shape[-1]
    along_y = jnp.einsum("...xy,yk->...xk", values, smooth_matrix(cols), precision=high)
    return jnp.einsum("...xy,kx->...ky", along_y, smooth_matrix(rows), precision=high)


def smooth(values, axis):
    total = KERNEL[2] * values
    for k in (1, 2):
        total = total + KERNEL[2 + k] * (shifted(values, axis, k) + shifted(values, axis, -k))
    return total


def exchange(fields, dim):
    devices = lax.axis_size("depth")
    length = fields[0].shape[dim]
    up = [(i, i + 1) for i in range(devices - 1)]
    down = [(i + 1, i) for i in range(devices - 1)]
    last = tuple(lax.slice_in_dim(f, length - HALO, length, axis=dim) for f in fields)
    leading = tuple(lax.slice_in_dim(f, 0, HALO, axis=dim) for f in fields)
    below = lax.ppermute(last, "depth", up)
    above = lax.ppermute(leading, "depth", down)
    return below, above


def spread(flat, values, first_plane, planes, rows, cols):
    lateral = rows * cols
    limit = planes * lateral
    local = flat - first_plane * lateral
    local = jnp.where((local >= 0) & (local < limit), local, limit)
    grid = jnp.zeros((values.shape[0], limit), jnp.float32).at[:, local].add(values, mode="drop")
    return grid.reshape(values.shape[0], planes, rows, cols)


def spread_dense(depth, cell, values, first_plane, planes, rows, cols):
    steps, count = values.shape
    local = depth - first_plane
    inside = (local >= 0) & (local < planes)
    row_id = jnp.where(inside, local * rows + cell // cols, -1)
    by_row = (row_id[None, :] == jnp.arange(planes * rows)[:, None]).astype(jnp.bfloat16)
    by_col = (cell % cols)[:, None] == jnp.arange(cols)[None, :]
    pieces = []
    rest = values
    for _ in range(3):
        piece = lax.reduce_precision(rest, exponent_bits=8, mantissa_bits=7)
        rest = rest - piece
        pieces.append(piece.astype(jnp.bfloat16))
    stacked = jnp.stack(pieces)
    right = jnp.where(by_col[None, None], stacked[:, :, :, None], jnp.zeros((), jnp.bfloat16))
    right = right.transpose(2, 0, 1, 3).reshape(count, 3 * steps * cols)
    grid = jnp.dot(by_row, right, preferred_element_type=jnp.float32)
    grid = grid.reshape(planes * rows, 3, steps, cols)
    grid = grid[:, 0] + grid[:, 1] + grid[:, 2]
    return grid.transpose(1, 0, 2).reshape(steps, planes, rows, cols)


def reduce_shots(values, dim):
    devices = lax.axis_size("shots")
    me = lax.axis_index("shots")
    length = values.shape[dim]
    shape = values.shape
    blocks = values.reshape(shape[:dim] + (devices, length // devices) + shape[dim + 1 :])
    bit = 1
    while bit < devices:
        count = blocks.shape[dim]
        paired = blocks.reshape(shape[:dim] + (count // 2, 2, length // devices) + shape[dim + 1 :])
        mine = (me // bit) % 2
        keep = lax.dynamic_index_in_dim(paired, mine, axis=dim + 1, keepdims=False)
        send = lax.dynamic_index_in_dim(paired, 1 - mine, axis=dim + 1, keepdims=False)
        pairs = [(i, i ^ bit) for i in range(devices)]
        blocks = keep + lax.ppermute(send, "shots", pairs)
        bit *= 2
    return blocks.reshape(shape[:dim] + (length // devices,) + shape[dim + 1 :])


def on_device(
    forward_prev,
    forward_now,
    adjoint_prev,
    adjoint_now,
    courant,
    wavelet,
    sign_bits,
    source_depth,
    source_cell,
    receiver_depth,
    receiver_cell,
    residual_traces,
):
    planes, rows, cols = courant.shape
    lateral = rows * cols
    source_flat = source_depth * lateral + source_cell
    receiver_flat = receiver_depth * lateral + receiver_cell
    signs = (2 * sign_bits - 1).astype(jnp.float32)
    position = lax.axis_index("depth")
    earlier = [forward_prev, adjoint_prev]
    current = [forward_now, adjoint_now]
    zaxis = 1
    below, above = exchange(current, zaxis)
    first_plane = position * planes
    correlation = None
    forward_terms = spread_dense(source_depth, source_cell, signs[0][None, :] * wavelet, first_plane, planes, rows, cols)
    adjoint_terms = spread_dense(receiver_depth, receiver_cell, residual_traces[0], first_plane, planes, rows, cols)
    for step in range(STEPS):
        terms = [forward_terms[step : step + 1], adjoint_terms[step : step + 1]]
        partial = lax.optimization_barrier(
            [
                2.0 * current[i] - earlier[i] + courant * lateral_laplace(current[i], zaxis) + terms[i]
                for i in range(2)
            ]
        )
        fresh = [
            partial[i] + courant * depth_laplace(below[i], current[i], above[i], zaxis) for i in range(2)
        ]
        if step + 1 < STEPS:
            below, above = exchange(fresh, zaxis)
        part = fresh[0][0] * fresh[1][0]
        correlation = part if correlation is None else correlation + part
        earlier, current = (current, fresh)
    lateral_smooth = smooth_lateral(correlation)
    reduced = reduce_shots(lateral_smooth, 1)
    columns = lax.all_to_all(reduced, "depth", split_axis=1, concat_axis=0, tiled=True)
    gradient = smooth(columns, 0)
    return (earlier[0], current[0], earlier[1], current[1], gradient)


def solution(mesh):
    in_specs = (
        P("shots", "depth", None, None),
        P("shots", "depth", None, None),
        P("shots", "depth", None, None),
        P("shots", "depth", None, None),
        P("depth", None, None),
        P(),
        P("shots", None),
        P(),
        P(),
        P(),
        P(),
        P("shots", None, None),
    )
    out_specs = (
        P("shots", "depth", None, None),
        P("shots", "depth", None, None),
        P("shots", "depth", None, None),
        P("shots", "depth", None, None),
        P(None, ("shots", "depth"), None),
    )
    return jax.shard_map(
        on_device, mesh=mesh, in_specs=in_specs, out_specs=out_specs, check_vma=False
    )
```

```python
import jax
import jax.numpy as jnp
from jax import lax
from jax.sharding import PartitionSpec as P

STEPS = 2
HALO = 4


COEFFS = (-205.0 / 72.0, 8.0 / 5.0, -1.0 / 5.0, 8.0 / 315.0, -1.0 / 560.0)
KERNEL = (1.0 / 16.0, 4.0 / 16.0, 6.0 / 16.0, 4.0 / 16.0, 1.0 / 16.0)


def shifted(values, axis, offset):
    size = values.shape[axis]
    width = abs(offset)
    pads = [(0, 0, 0)] * values.ndim
    if offset > 0:
        kept = lax.slice_in_dim(values, offset, size, axis=axis)
        pads[axis] = (0, width, 0)
    else:
        kept = lax.slice_in_dim(values, 0, size - width, axis=axis)
        pads[axis] = (width, 0, 0)
    return lax.pad(kept, jnp.array(0.0, values.dtype), pads)


def band(size):
    index = jnp.arange(size)
    gap = jnp.abs(index[:, None] - index[None, :])
    matrix = jnp.zeros((size, size), jnp.float32)
    for k in range(1, 5):
        matrix = jnp.where(gap == k, jnp.float32(COEFFS[k]), matrix)
    return matrix


def lateral_laplace(core, zaxis):
    rows, cols = core.shape[zaxis + 1], core.shape[zaxis + 2]
    high = lax.Precision.HIGHEST
    along_y = jnp.einsum("...xy,yk->...xk", core, band(cols), precision=high)
    along_x = jnp.einsum("...xy,kx->...ky", core, band(rows), precision=high)
    return 3.0 * COEFFS[0] * core + (along_x + along_y)


def depth_laplace(below, core, above, zaxis):
    planes = core.shape[zaxis]
    extended = jnp.concatenate([below, core, above], axis=zaxis)
    total = None
    for k in range(1, 5):
        near = lax.slice_in_dim(extended, HALO + k, HALO + k + planes, axis=zaxis) + lax.slice_in_dim(
            extended, HALO - k, HALO - k + planes, axis=zaxis
        )
        total = COEFFS[k] * near if total is None else total + COEFFS[k] * near
    return total


def smooth_matrix(size):
    index = jnp.arange(size)
    gap = index[:, None] - index[None, :]
    matrix = jnp.zeros((size, size), jnp.float32)
    for k in range(-2, 3):
        matrix = jnp.where(gap == k, jnp.float32(KERNEL[2 + k]), matrix)
    return matrix


def smooth_lateral(values):
    high = lax.Precision.HIGHEST
    rows, cols = values.shape[-2], values.shape[-1]
    along_y = jnp.einsum("...xy,yk->...xk", values, smooth_matrix(cols), precision=high)
    return jnp.einsum("...xy,kx->...ky", along_y, smooth_matrix(rows), precision=high)


def smooth(values, axis):
    total = KERNEL[2] * values
    for k in (1, 2):
        total = total + KERNEL[2 + k] * (shifted(values, axis, k) + shifted(values, axis, -k))
    return total


def exchange(fields, dim):
    devices = lax.axis_size("depth")
    length = fields[0].shape[dim]
    up = [(i, i + 1) for i in range(devices - 1)]
    down = [(i + 1, i) for i in range(devices - 1)]
    below, above = [], []
    for f in fields:
        below.append(lax.ppermute(lax.slice_in_dim(f, length - HALO, length, axis=dim), "depth", up))
        above.append(lax.ppermute(lax.slice_in_dim(f, 0, HALO, axis=dim), "depth", down))
    return below, above


def spread(flat, values, first_plane, planes, rows, cols):
    lateral = rows * cols
    limit = planes * lateral
    local = flat - first_plane * lateral
    local = jnp.where((local >= 0) & (local < limit), local, limit)
    grid = jnp.zeros((values.shape[0], limit), jnp.float32).at[:, local].add(values, mode="drop")
    return grid.reshape(values.shape[0], planes, rows, cols)


def spread_dense(depth, cell, values, first_plane, planes, rows, cols):
    steps, count = values.shape
    local = depth - first_plane
    inside = (local >= 0) & (local < planes)
    row_id = jnp.where(inside, local * rows + cell // cols, -1)
    by_row = (row_id[None, :] == jnp.arange(planes * rows)[:, None]).astype(jnp.bfloat16)
    by_col = (cell % cols)[:, None] == jnp.arange(cols)[None, :]
    pieces = []
    rest = values
    for _ in range(3):
        piece = lax.reduce_precision(rest, exponent_bits=8, mantissa_bits=7)
        rest = rest - piece
        pieces.append(piece.astype(jnp.bfloat16))
    stacked = jnp.stack(pieces)
    right = jnp.where(by_col[None, None], stacked[:, :, :, None], jnp.zeros((), jnp.bfloat16))
    right = right.transpose(2, 0, 1, 3).reshape(count, 3 * steps * cols)
    grid = jnp.dot(by_row, right, preferred_element_type=jnp.float32)
    grid = grid.reshape(planes * rows, 3, steps, cols)
    grid = grid[:, 0] + grid[:, 1] + grid[:, 2]
    return grid.transpose(1, 0, 2).reshape(steps, planes, rows, cols)


def reduce_shots(values, dim):
    devices = lax.axis_size("shots")
    me = lax.axis_index("shots")
    length = values.shape[dim]
    shape = values.shape
    blocks = values.reshape(shape[:dim] + (devices, length // devices) + shape[dim + 1 :])
    bit = 1
    while bit < devices:
        count = blocks.shape[dim]
        paired = blocks.reshape(shape[:dim] + (count // 2, 2, length // devices) + shape[dim + 1 :])
        mine = (me // bit) % 2
        keep = lax.dynamic_index_in_dim(paired, mine, axis=dim + 1, keepdims=False)
        send = lax.dynamic_index_in_dim(paired, 1 - mine, axis=dim + 1, keepdims=False)
        pairs = [(i, i ^ bit) for i in range(devices)]
        blocks = keep + lax.ppermute(send, "shots", pairs)
        bit *= 2
    return blocks.reshape(shape[:dim] + (length // devices,) + shape[dim + 1 :])


def on_device(
    forward_prev,
    forward_now,
    adjoint_prev,
    adjoint_now,
    courant,
    wavelet,
    sign_bits,
    source_depth,
    source_cell,
    receiver_depth,
    receiver_cell,
    residual_traces,
):
    planes, rows, cols = courant.shape
    lateral = rows * cols
    source_flat = source_depth * lateral + source_cell
    receiver_flat = receiver_depth * lateral + receiver_cell
    signs = (2 * sign_bits - 1).astype(jnp.float32)
    position = lax.axis_index("depth")
    earlier = [forward_prev, adjoint_prev]
    current = [forward_now, adjoint_now]
    zaxis = 1
    below, above = exchange(current, zaxis)
    first_plane = position * planes
    correlation = None
    forward_terms = spread_dense(source_depth, source_cell, signs[0][None, :] * wavelet, first_plane, planes, rows, cols)
    adjoint_terms = spread_dense(receiver_depth, receiver_cell, residual_traces[0], first_plane, planes, rows, cols)
    for step in range(STEPS):
        terms = [forward_terms[step : step + 1], adjoint_terms[step : step + 1]]
        partial = lax.optimization_barrier(
            [
                2.0 * current[i] - earlier[i] + courant * lateral_laplace(current[i], zaxis) + terms[i]
                for i in range(2)
            ]
        )
        fresh = []
        halos = ([], [])
        for i in range(2):
            if i > 0 and step + 1 < STEPS:
                _, below[i], above[i] = lax.optimization_barrier((halos[0][-1], below[i], above[i]))
            fresh.append(partial[i] + courant * depth_laplace(below[i], current[i], above[i], zaxis))
            if step + 1 < STEPS:
                sent = exchange([fresh[i]], zaxis)
                halos[0].append(sent[0][0])
                halos[1].append(sent[1][0])
        if step + 1 < STEPS:
            below, above = halos
        part = fresh[0][0] * fresh[1][0]
        correlation = part if correlation is None else correlation + part
        earlier, current = (current, fresh)
    lateral_smooth = smooth_lateral(correlation)
    reduced = reduce_shots(lateral_smooth, 1)
    columns = lax.all_to_all(reduced, "depth", split_axis=1, concat_axis=0, tiled=True)
    gradient = smooth(columns, 0)
    return (earlier[0], current[0], earlier[1], current[1], gradient)


def solution(mesh):
    in_specs = (
        P("shots", "depth", None, None),
        P("shots", "depth", None, None),
        P("shots", "depth", None, None),
        P("shots", "depth", None, None),
        P("depth", None, None),
        P(),
        P("shots", None),
        P(),
        P(),
        P(),
        P(),
        P("shots", None, None),
    )
    out_specs = (
        P("shots", "depth", None, None),
        P("shots", "depth", None, None),
        P("shots", "depth", None, None),
        P("shots", "depth", None, None),
        P(None, ("shots", "depth"), None),
    )
    return jax.shard_map(
        on_device, mesh=mesh, in_specs=in_specs, out_specs=out_specs, check_vma=False
    )
```

```python
import jax
import jax.numpy as jnp
from jax import lax
from jax.sharding import PartitionSpec as P

STEPS = 2
HALO = 4


COEFFS = (-205.0 / 72.0, 8.0 / 5.0, -1.0 / 5.0, 8.0 / 315.0, -1.0 / 560.0)
KERNEL = (1.0 / 16.0, 4.0 / 16.0, 6.0 / 16.0, 4.0 / 16.0, 1.0 / 16.0)


def shifted(values, axis, offset):
    size = values.shape[axis]
    width = abs(offset)
    pads = [(0, 0, 0)] * values.ndim
    if offset > 0:
        kept = lax.slice_in_dim(values, offset, size, axis=axis)
        pads[axis] = (0, width, 0)
    else:
        kept = lax.slice_in_dim(values, 0, size - width, axis=axis)
        pads[axis] = (width, 0, 0)
    return lax.pad(kept, jnp.array(0.0, values.dtype), pads)


def band(size):
    index = jnp.arange(size)
    gap = jnp.abs(index[:, None] - index[None, :])
    matrix = jnp.zeros((size, size), jnp.float32)
    for k in range(1, 5):
        matrix = jnp.where(gap == k, jnp.float32(COEFFS[k]), matrix)
    return matrix


def lateral_laplace(core, zaxis):
    rows, cols = core.shape[zaxis + 1], core.shape[zaxis + 2]
    high = lax.Precision.HIGHEST
    along_y = jnp.einsum("...xy,yk->...xk", core, band(cols), precision=high)
    along_x = jnp.einsum("...xy,kx->...ky", core, band(rows), precision=high)
    return 3.0 * COEFFS[0] * core + (along_x + along_y)


def depth_laplace(below, core, above, zaxis):
    planes = core.shape[zaxis]
    extended = jnp.concatenate([below, core, above], axis=zaxis)
    total = None
    for k in range(1, 5):
        near = lax.slice_in_dim(extended, HALO + k, HALO + k + planes, axis=zaxis) + lax.slice_in_dim(
            extended, HALO - k, HALO - k + planes, axis=zaxis
        )
        total = COEFFS[k] * near if total is None else total + COEFFS[k] * near
    return total


def smooth_matrix(size):
    index = jnp.arange(size)
    gap = index[:, None] - index[None, :]
    matrix = jnp.zeros((size, size), jnp.float32)
    for k in range(-2, 3):
        matrix = jnp.where(gap == k, jnp.float32(KERNEL[2 + k]), matrix)
    return matrix


def smooth_lateral(values):
    high = lax.Precision.HIGHEST
    rows, cols = values.shape[-2], values.shape[-1]
    along_y = jnp.einsum("...xy,yk->...xk", values, smooth_matrix(cols), precision=high)
    return jnp.einsum("...xy,kx->...ky", along_y, smooth_matrix(rows), precision=high)


def smooth(values, axis):
    total = KERNEL[2] * values
    for k in (1, 2):
        total = total + KERNEL[2 + k] * (shifted(values, axis, k) + shifted(values, axis, -k))
    return total


def exchange(fields, dim):
    devices = lax.axis_size("depth")
    length = fields[0].shape[dim]
    up = [(i, i + 1) for i in range(devices - 1)]
    down = [(i + 1, i) for i in range(devices - 1)]
    below, above = [], []
    for f in fields:
        below.append(lax.ppermute(lax.slice_in_dim(f, length - HALO, length, axis=dim), "depth", up))
        above.append(lax.ppermute(lax.slice_in_dim(f, 0, HALO, axis=dim), "depth", down))
    return below, above


def spread(flat, values, first_plane, planes, rows, cols):
    lateral = rows * cols
    limit = planes * lateral
    local = flat - first_plane * lateral
    local = jnp.where((local >= 0) & (local < limit), local, limit)
    grid = jnp.zeros((values.shape[0], limit), jnp.float32).at[:, local].add(values, mode="drop")
    return grid.reshape(values.shape[0], planes, rows, cols)


def spread_dense(depth, cell, values, first_plane, planes, rows, cols):
    steps, count = values.shape
    local = depth - first_plane
    inside = (local >= 0) & (local < planes)
    row_id = jnp.where(inside, local * rows + cell // cols, -1)
    by_row = (row_id[None, :] == jnp.arange(planes * rows)[:, None]).astype(jnp.bfloat16)
    by_col = (cell % cols)[:, None] == jnp.arange(cols)[None, :]
    pieces = []
    rest = values
    for _ in range(3):
        piece = lax.reduce_precision(rest, exponent_bits=8, mantissa_bits=7)
        rest = rest - piece
        pieces.append(piece.astype(jnp.bfloat16))
    stacked = jnp.stack(pieces)
    right = jnp.where(by_col[None, None], stacked[:, :, :, None], jnp.zeros((), jnp.bfloat16))
    right = right.transpose(2, 0, 1, 3).reshape(count, 3 * steps * cols)
    grid = jnp.dot(by_row, right, preferred_element_type=jnp.float32)
    grid = grid.reshape(planes * rows, 3, steps, cols)
    grid = grid[:, 0] + grid[:, 1] + grid[:, 2]
    return grid.transpose(1, 0, 2).reshape(steps, planes, rows, cols)


def reduce_shots(values, dim):
    devices = lax.axis_size("shots")
    me = lax.axis_index("shots")
    length = values.shape[dim]
    shape = values.shape
    blocks = values.reshape(shape[:dim] + (devices, length // devices) + shape[dim + 1 :])
    bit = 1
    while bit < devices:
        count = blocks.shape[dim]
        paired = blocks.reshape(shape[:dim] + (count // 2, 2, length // devices) + shape[dim + 1 :])
        mine = (me // bit) % 2
        keep = lax.dynamic_index_in_dim(paired, mine, axis=dim + 1, keepdims=False)
        send = lax.dynamic_index_in_dim(paired, 1 - mine, axis=dim + 1, keepdims=False)
        pairs = [(i, i ^ bit) for i in range(devices)]
        blocks = keep + lax.ppermute(send, "shots", pairs)
        bit *= 2
    return blocks.reshape(shape[:dim] + (length // devices,) + shape[dim + 1 :])


def on_device(
    forward_prev,
    forward_now,
    adjoint_prev,
    adjoint_now,
    courant,
    wavelet,
    sign_bits,
    source_depth,
    source_cell,
    receiver_depth,
    receiver_cell,
    residual_traces,
):
    planes, rows, cols = courant.shape
    lateral = rows * cols
    source_flat = source_depth * lateral + source_cell
    receiver_flat = receiver_depth * lateral + receiver_cell
    signs = (2 * sign_bits - 1).astype(jnp.float32)
    position = lax.axis_index("depth")
    earlier = [forward_prev, adjoint_prev]
    current = [forward_now, adjoint_now]
    zaxis = 1
    below, above = exchange(current, zaxis)
    first_plane = position * planes
    correlation = None
    forward_terms = spread_dense(source_depth, source_cell, signs[0][None, :] * wavelet, first_plane, planes, rows, cols)
    adjoint_terms = spread_dense(receiver_depth, receiver_cell, residual_traces[0], first_plane, planes, rows, cols)
    for step in range(STEPS):
        terms = [forward_terms[step : step + 1], adjoint_terms[step : step + 1]]
        partial = lax.optimization_barrier(
            [
                2.0 * current[i] - earlier[i] + courant * lateral_laplace(current[i], zaxis) + terms[i]
                for i in range(2)
            ]
        )
        fresh = []
        halos = ([], [])
        for i in range(2):
            if i > 0 and step + 1 < STEPS:
                _, below[i], above[i] = lax.optimization_barrier((marker, below[i], above[i]))
            fresh.append(partial[i] + courant * depth_laplace(below[i], current[i], above[i], zaxis))
            if step + 1 < STEPS:
                if i == 0:
                    devices = lax.axis_size("depth")
                    length = fresh[i].shape[zaxis]
                    marker = lax.ppermute(
                        lax.slice_in_dim(fresh[i], length - 1, length, axis=zaxis),
                        "depth",
                        [(j, j + 1) for j in range(devices - 1)],
                    )
                    rest = lax.ppermute(
                        lax.slice_in_dim(fresh[i], length - HALO, length - 1, axis=zaxis),
                        "depth",
                        [(j, j + 1) for j in range(devices - 1)],
                    )
                    leading = lax.ppermute(
                        lax.slice_in_dim(fresh[i], 0, HALO, axis=zaxis),
                        "depth",
                        [(j + 1, j) for j in range(devices - 1)],
                    )
                    halos[0].append(jnp.concatenate([rest, marker], axis=zaxis))
                    halos[1].append(leading)
                else:
                    sent = exchange([fresh[i]], zaxis)
                    halos[0].append(sent[0][0])
                    halos[1].append(sent[1][0])
        if step + 1 < STEPS:
            below, above = halos
        part = fresh[0][0] * fresh[1][0]
        correlation = part if correlation is None else correlation + part
        earlier, current = (current, fresh)
    lateral_smooth = smooth_lateral(correlation)
    reduced = reduce_shots(lateral_smooth, 1)
    columns = lax.all_to_all(reduced, "depth", split_axis=1, concat_axis=0, tiled=True)
    gradient = smooth(columns, 0)
    return (earlier[0], current[0], earlier[1], current[1], gradient)


def solution(mesh):
    in_specs = (
        P("shots", "depth", None, None),
        P("shots", "depth", None, None),
        P("shots", "depth", None, None),
        P("shots", "depth", None, None),
        P("depth", None, None),
        P(),
        P("shots", None),
        P(),
        P(),
        P(),
        P(),
        P("shots", None, None),
    )
    out_specs = (
        P("shots", "depth", None, None),
        P("shots", "depth", None, None),
        P("shots", "depth", None, None),
        P("shots", "depth", None, None),
        P(None, ("shots", "depth"), None),
    )
    return jax.shard_map(
        on_device, mesh=mesh, in_specs=in_specs, out_specs=out_specs, check_vma=False
    )
```

```python
import jax
import jax.numpy as jnp
from jax import lax
from jax.sharding import PartitionSpec as P

STEPS = 2
HALO = 4


COEFFS = (-205.0 / 72.0, 8.0 / 5.0, -1.0 / 5.0, 8.0 / 315.0, -1.0 / 560.0)
KERNEL = (1.0 / 16.0, 4.0 / 16.0, 6.0 / 16.0, 4.0 / 16.0, 1.0 / 16.0)


def shifted(values, axis, offset):
    size = values.shape[axis]
    width = abs(offset)
    pads = [(0, 0, 0)] * values.ndim
    if offset > 0:
        kept = lax.slice_in_dim(values, offset, size, axis=axis)
        pads[axis] = (0, width, 0)
    else:
        kept = lax.slice_in_dim(values, 0, size - width, axis=axis)
        pads[axis] = (width, 0, 0)
    return lax.pad(kept, jnp.array(0.0, values.dtype), pads)


def band(size):
    index = jnp.arange(size)
    gap = jnp.abs(index[:, None] - index[None, :])
    matrix = jnp.zeros((size, size), jnp.float32)
    for k in range(1, 5):
        matrix = jnp.where(gap == k, jnp.float32(COEFFS[k]), matrix)
    return matrix


def lateral_laplace(core, zaxis):
    rows, cols = core.shape[zaxis + 1], core.shape[zaxis + 2]
    high = lax.Precision.HIGHEST
    along_y = jnp.einsum("...xy,yk->...xk", core, band(cols), precision=high)
    along_x = jnp.einsum("...xy,kx->...ky", core, band(rows), precision=high)
    return 3.0 * COEFFS[0] * core + (along_x + along_y)


def depth_laplace(below, core, above, zaxis):
    planes = core.shape[zaxis]
    extended = jnp.concatenate([below, core, above], axis=zaxis)
    total = None
    for k in range(1, 5):
        near = lax.slice_in_dim(extended, HALO + k, HALO + k + planes, axis=zaxis) + lax.slice_in_dim(
            extended, HALO - k, HALO - k + planes, axis=zaxis
        )
        total = COEFFS[k] * near if total is None else total + COEFFS[k] * near
    return total


def smooth_matrix(size):
    index = jnp.arange(size)
    gap = index[:, None] - index[None, :]
    matrix = jnp.zeros((size, size), jnp.float32)
    for k in range(-2, 3):
        matrix = jnp.where(gap == k, jnp.float32(KERNEL[2 + k]), matrix)
    return matrix


def smooth_lateral(values):
    high = lax.Precision.HIGHEST
    rows, cols = values.shape[-2], values.shape[-1]
    along_y = jnp.einsum("...xy,yk->...xk", values, smooth_matrix(cols), precision=high)
    return jnp.einsum("...xy,kx->...ky", along_y, smooth_matrix(rows), precision=high)


def smooth(values, axis):
    total = KERNEL[2] * values
    for k in (1, 2):
        total = total + KERNEL[2 + k] * (shifted(values, axis, k) + shifted(values, axis, -k))
    return total


def exchange(fields, dim):
    devices = lax.axis_size("depth")
    length = fields[0].shape[dim]
    up = [(i, i + 1) for i in range(devices - 1)]
    down = [(i + 1, i) for i in range(devices - 1)]
    below, above = [], []
    for f in fields:
        below.append(lax.ppermute(lax.slice_in_dim(f, length - HALO, length, axis=dim), "depth", up))
        above.append(lax.ppermute(lax.slice_in_dim(f, 0, HALO, axis=dim), "depth", down))
    return below, above


def spread(flat, values, first_plane, planes, rows, cols):
    lateral = rows * cols
    limit = planes * lateral
    local = flat - first_plane * lateral
    local = jnp.where((local >= 0) & (local < limit), local, limit)
    grid = jnp.zeros((values.shape[0], limit), jnp.float32).at[:, local].add(values, mode="drop")
    return grid.reshape(values.shape[0], planes, rows, cols)


def spread_dense(depth, cell, values, first_plane, planes, rows, cols):
    steps, count = values.shape
    local = depth - first_plane
    inside = (local >= 0) & (local < planes)
    row_id = jnp.where(inside, local * rows + cell // cols, -1)
    by_row = (row_id[None, :] == jnp.arange(planes * rows)[:, None]).astype(jnp.bfloat16)
    by_col = (cell % cols)[:, None] == jnp.arange(cols)[None, :]
    pieces = []
    rest = values
    for _ in range(3):
        piece = lax.reduce_precision(rest, exponent_bits=8, mantissa_bits=7)
        rest = rest - piece
        pieces.append(piece.astype(jnp.bfloat16))
    stacked = jnp.stack(pieces)
    right = jnp.where(by_col[None, None], stacked[:, :, :, None], jnp.zeros((), jnp.bfloat16))
    right = right.transpose(2, 0, 1, 3).reshape(count, 3 * steps * cols)
    grid = jnp.dot(by_row, right, preferred_element_type=jnp.float32)
    grid = grid.reshape(planes * rows, 3, steps, cols)
    grid = grid[:, 0] + grid[:, 1] + grid[:, 2]
    return grid.transpose(1, 0, 2).reshape(steps, planes, rows, cols)


def reduce_shots(values, dim):
    devices = lax.axis_size("shots")
    me = lax.axis_index("shots")
    length = values.shape[dim]
    shape = values.shape
    blocks = values.reshape(shape[:dim] + (devices, length // devices) + shape[dim + 1 :])
    bit = 1
    while bit < devices:
        count = blocks.shape[dim]
        paired = blocks.reshape(shape[:dim] + (count // 2, 2, length // devices) + shape[dim + 1 :])
        mine = (me // bit) % 2
        keep = lax.dynamic_index_in_dim(paired, mine, axis=dim + 1, keepdims=False)
        send = lax.dynamic_index_in_dim(paired, 1 - mine, axis=dim + 1, keepdims=False)
        pairs = [(i, i ^ bit) for i in range(devices)]
        blocks = keep + lax.ppermute(send, "shots", pairs)
        bit *= 2
    return blocks.reshape(shape[:dim] + (length // devices,) + shape[dim + 1 :])


def on_device(
    forward_prev,
    forward_now,
    adjoint_prev,
    adjoint_now,
    courant,
    wavelet,
    sign_bits,
    source_depth,
    source_cell,
    receiver_depth,
    receiver_cell,
    residual_traces,
):
    planes, rows, cols = courant.shape
    lateral = rows * cols
    source_flat = source_depth * lateral + source_cell
    receiver_flat = receiver_depth * lateral + receiver_cell
    signs = (2 * sign_bits - 1).astype(jnp.float32)
    position = lax.axis_index("depth")
    earlier = [forward_prev, adjoint_prev]
    current = [forward_now, adjoint_now]
    zaxis = 1
    below, above = exchange(current, zaxis)
    first_plane = position * planes
    correlation = None
    forward_terms = spread_dense(source_depth, source_cell, signs[0][None, :] * wavelet, first_plane, planes, rows, cols)
    adjoint_terms = spread_dense(receiver_depth, receiver_cell, residual_traces[0], first_plane, planes, rows, cols)
    markers = []
    for step in range(STEPS):
        terms = [forward_terms[step : step + 1], adjoint_terms[step : step + 1]]
        if markers:
            _, current[1] = lax.optimization_barrier((markers[1], current[1]))
        partial = lax.optimization_barrier(
            [
                2.0 * current[i] - earlier[i] + courant * lateral_laplace(current[i], zaxis) + terms[i]
                for i in range(2)
            ]
        )
        fresh = []
        halos = ([], [])
        markers = []
        for i in range(2):
            if i > 0 and step + 1 < STEPS:
                _, below[i], above[i] = lax.optimization_barrier((markers[0], below[i], above[i]))
            fresh.append(partial[i] + courant * depth_laplace(below[i], current[i], above[i], zaxis))
            if step + 1 < STEPS:
                devices = lax.axis_size("depth")
                length = fresh[i].shape[zaxis]
                marker = lax.ppermute(
                    lax.slice_in_dim(fresh[i], length - 1, length, axis=zaxis),
                    "depth",
                    [(j, j + 1) for j in range(devices - 1)],
                )
                rest = lax.ppermute(
                    lax.slice_in_dim(fresh[i], length - HALO, length - 1, axis=zaxis),
                    "depth",
                    [(j, j + 1) for j in range(devices - 1)],
                )
                leading = lax.ppermute(
                    lax.slice_in_dim(fresh[i], 0, HALO, axis=zaxis),
                    "depth",
                    [(j + 1, j) for j in range(devices - 1)],
                )
                halos[0].append(jnp.concatenate([rest, marker], axis=zaxis))
                halos[1].append(leading)
                markers.append(marker)
        if step + 1 < STEPS:
            below, above = halos
        part = fresh[0][0] * fresh[1][0]
        correlation = part if correlation is None else correlation + part
        earlier, current = (current, fresh)
    lateral_smooth = smooth_lateral(correlation)
    reduced = reduce_shots(lateral_smooth, 1)
    columns = lax.all_to_all(reduced, "depth", split_axis=1, concat_axis=0, tiled=True)
    gradient = smooth(columns, 0)
    return (earlier[0], current[0], earlier[1], current[1], gradient)


def solution(mesh):
    in_specs = (
        P("shots", "depth", None, None),
        P("shots", "depth", None, None),
        P("shots", "depth", None, None),
        P("shots", "depth", None, None),
        P("depth", None, None),
        P(),
        P("shots", None),
        P(),
        P(),
        P(),
        P(),
        P("shots", None, None),
    )
    out_specs = (
        P("shots", "depth", None, None),
        P("shots", "depth", None, None),
        P("shots", "depth", None, None),
        P("shots", "depth", None, None),
        P(None, ("shots", "depth"), None),
    )
    return jax.shard_map(
        on_device, mesh=mesh, in_specs=in_specs, out_specs=out_specs, check_vma=False
    )
```

```python
import jax
import jax.numpy as jnp
from jax import lax
from jax.sharding import PartitionSpec as P

STEPS = 2
HALO = 4


COEFFS = (-205.0 / 72.0, 8.0 / 5.0, -1.0 / 5.0, 8.0 / 315.0, -1.0 / 560.0)
KERNEL = (1.0 / 16.0, 4.0 / 16.0, 6.0 / 16.0, 4.0 / 16.0, 1.0 / 16.0)


def shifted(values, axis, offset):
    size = values.shape[axis]
    width = abs(offset)
    pads = [(0, 0, 0)] * values.ndim
    if offset > 0:
        kept = lax.slice_in_dim(values, offset, size, axis=axis)
        pads[axis] = (0, width, 0)
    else:
        kept = lax.slice_in_dim(values, 0, size - width, axis=axis)
        pads[axis] = (width, 0, 0)
    return lax.pad(kept, jnp.array(0.0, values.dtype), pads)


def band(size):
    index = jnp.arange(size)
    gap = jnp.abs(index[:, None] - index[None, :])
    matrix = jnp.zeros((size, size), jnp.float32)
    for k in range(1, 5):
        matrix = jnp.where(gap == k, jnp.float32(COEFFS[k]), matrix)
    return matrix


def lateral_laplace(core, zaxis):
    rows, cols = core.shape[zaxis + 1], core.shape[zaxis + 2]
    high = lax.Precision.HIGHEST
    along_y = jnp.einsum("...xy,yk->...xk", core, band(cols), precision=high)
    along_x = jnp.einsum("...xy,kx->...ky", core, band(rows), precision=high)
    return 3.0 * COEFFS[0] * core + (along_x + along_y)


def depth_laplace(below, core, above, zaxis):
    planes = core.shape[zaxis]
    extended = jnp.concatenate([below, core, above], axis=zaxis)
    total = None
    for k in range(1, 5):
        near = lax.slice_in_dim(extended, HALO + k, HALO + k + planes, axis=zaxis) + lax.slice_in_dim(
            extended, HALO - k, HALO - k + planes, axis=zaxis
        )
        total = COEFFS[k] * near if total is None else total + COEFFS[k] * near
    return total


def smooth_matrix(size):
    index = jnp.arange(size)
    gap = index[:, None] - index[None, :]
    matrix = jnp.zeros((size, size), jnp.float32)
    for k in range(-2, 3):
        matrix = jnp.where(gap == k, jnp.float32(KERNEL[2 + k]), matrix)
    return matrix


def smooth_lateral(values):
    high = lax.Precision.HIGHEST
    rows, cols = values.shape[-2], values.shape[-1]
    along_y = jnp.einsum("...xy,yk->...xk", values, smooth_matrix(cols), precision=high)
    return jnp.einsum("...xy,kx->...ky", along_y, smooth_matrix(rows), precision=high)


def smooth(values, axis):
    total = KERNEL[2] * values
    for k in (1, 2):
        total = total + KERNEL[2 + k] * (shifted(values, axis, k) + shifted(values, axis, -k))
    return total


def exchange(fields, dim):
    devices = lax.axis_size("depth")
    length = fields[0].shape[dim]
    up = [(i, i + 1) for i in range(devices - 1)]
    down = [(i + 1, i) for i in range(devices - 1)]
    below, above = [], []
    for f in fields:
        below.append(lax.ppermute(lax.slice_in_dim(f, length - HALO, length, axis=dim), "depth", up))
        above.append(lax.ppermute(lax.slice_in_dim(f, 0, HALO, axis=dim), "depth", down))
    return below, above


def spread(flat, values, first_plane, planes, rows, cols):
    lateral = rows * cols
    limit = planes * lateral
    local = flat - first_plane * lateral
    local = jnp.where((local >= 0) & (local < limit), local, limit)
    grid = jnp.zeros((values.shape[0], limit), jnp.float32).at[:, local].add(values, mode="drop")
    return grid.reshape(values.shape[0], planes, rows, cols)


def spread_dense(depth, cell, values, first_plane, planes, rows, cols):
    steps, count = values.shape
    local = depth - first_plane
    inside = (local >= 0) & (local < planes)
    row_id = jnp.where(inside, local * rows + cell // cols, -1)
    by_row = (row_id[None, :] == jnp.arange(planes * rows)[:, None]).astype(jnp.bfloat16)
    by_col = (cell % cols)[:, None] == jnp.arange(cols)[None, :]
    pieces = []
    rest = values
    for _ in range(3):
        piece = lax.reduce_precision(rest, exponent_bits=8, mantissa_bits=7)
        rest = rest - piece
        pieces.append(piece.astype(jnp.bfloat16))
    stacked = jnp.stack(pieces)
    right = jnp.where(by_col[None, None], stacked[:, :, :, None], jnp.zeros((), jnp.bfloat16))
    right = right.transpose(2, 0, 1, 3).reshape(count, 3 * steps * cols)
    grid = jnp.dot(by_row, right, preferred_element_type=jnp.float32)
    grid = grid.reshape(planes * rows, 3, steps, cols)
    grid = grid[:, 0] + grid[:, 1] + grid[:, 2]
    return grid.transpose(1, 0, 2).reshape(steps, planes, rows, cols)


def reduce_shots(values, dim):
    devices = lax.axis_size("shots")
    me = lax.axis_index("shots")
    length = values.shape[dim]
    shape = values.shape
    blocks = values.reshape(shape[:dim] + (devices, length // devices) + shape[dim + 1 :])
    bit = 1
    while bit < devices:
        count = blocks.shape[dim]
        paired = blocks.reshape(shape[:dim] + (count // 2, 2, length // devices) + shape[dim + 1 :])
        mine = (me // bit) % 2
        keep = lax.dynamic_index_in_dim(paired, mine, axis=dim + 1, keepdims=False)
        send = lax.dynamic_index_in_dim(paired, 1 - mine, axis=dim + 1, keepdims=False)
        pairs = [(i, i ^ bit) for i in range(devices)]
        blocks = keep + lax.ppermute(send, "shots", pairs)
        bit *= 2
    return blocks.reshape(shape[:dim] + (length // devices,) + shape[dim + 1 :])


def on_device(
    forward_prev,
    forward_now,
    adjoint_prev,
    adjoint_now,
    courant,
    wavelet,
    sign_bits,
    source_depth,
    source_cell,
    receiver_depth,
    receiver_cell,
    residual_traces,
):
    planes, rows, cols = courant.shape
    lateral = rows * cols
    source_flat = source_depth * lateral + source_cell
    receiver_flat = receiver_depth * lateral + receiver_cell
    signs = (2 * sign_bits - 1).astype(jnp.float32)
    position = lax.axis_index("depth")
    earlier = [forward_prev, adjoint_prev]
    current = [forward_now, adjoint_now]
    zaxis = 1
    below, above = exchange(current, zaxis)
    first_plane = position * planes
    correlation = None
    forward_terms = spread_dense(source_depth, source_cell, signs[0][None, :] * wavelet, first_plane, planes, rows, cols)
    adjoint_terms = spread_dense(receiver_depth, receiver_cell, residual_traces[0], first_plane, planes, rows, cols)
    for step in range(STEPS):
        terms = [forward_terms[step : step + 1], adjoint_terms[step : step + 1]]
        partial = lax.optimization_barrier(
            [
                2.0 * current[i] - earlier[i] + courant * lateral_laplace(current[i], zaxis) + terms[i]
                for i in range(2)
            ]
        )
        fresh = []
        halos = ([], [])
        for i in range(2):
            if i > 0 and step + 1 < STEPS:
                _, below[i], above[i] = lax.optimization_barrier((marker, below[i], above[i]))
            fresh.append(partial[i] + courant * depth_laplace(below[i], current[i], above[i], zaxis))
            if step + 1 < STEPS:
                if i == 0:
                    devices = lax.axis_size("depth")
                    length = fresh[i].shape[zaxis]
                    marker = lax.ppermute(
                        lax.slice_in_dim(fresh[i], length - 1, length, axis=zaxis),
                        "depth",
                        [(j, j + 1) for j in range(devices - 1)],
                    )
                    rest = lax.ppermute(
                        lax.slice_in_dim(fresh[i], length - HALO, length - 1, axis=zaxis),
                        "depth",
                        [(j, j + 1) for j in range(devices - 1)],
                    )
                    leading = lax.ppermute(
                        lax.slice_in_dim(fresh[i], 0, HALO, axis=zaxis),
                        "depth",
                        [(j + 1, j) for j in range(devices - 1)],
                    )
                    halos[0].append(jnp.concatenate([rest, marker], axis=zaxis))
                    halos[1].append(leading)
                else:
                    sent = exchange([fresh[i]], zaxis)
                    halos[0].append(sent[0][0])
                    halos[1].append(sent[1][0])
        if step + 1 < STEPS:
            below, above = halos
        part = fresh[0][0] * fresh[1][0]
        correlation = part if correlation is None else correlation + part
        earlier, current = (current, fresh)
    lateral_smooth = smooth_lateral(correlation)
    reduced = reduce_shots(lateral_smooth, 1)
    columns = lax.all_to_all(reduced, "depth", split_axis=1, concat_axis=0, tiled=True)
    gradient = jnp.einsum("zw,wxy->zxy", smooth_matrix(columns.shape[0]), columns, precision=lax.Precision.HIGHEST)
    return (earlier[0], current[0], earlier[1], current[1], gradient)


def solution(mesh):
    in_specs = (
        P("shots", "depth", None, None),
        P("shots", "depth", None, None),
        P("shots", "depth", None, None),
        P("shots", "depth", None, None),
        P("depth", None, None),
        P(),
        P("shots", None),
        P(),
        P(),
        P(),
        P(),
        P("shots", None, None),
    )
    out_specs = (
        P("shots", "depth", None, None),
        P("shots", "depth", None, None),
        P("shots", "depth", None, None),
        P("shots", "depth", None, None),
        P(None, ("shots", "depth"), None),
    )
    return jax.shard_map(
        on_device, mesh=mesh, in_specs=in_specs, out_specs=out_specs, check_vma=False
    )
```

```python
import jax
import jax.numpy as jnp
from jax import lax
from jax.sharding import PartitionSpec as P

STEPS = 2
HALO = 4


COEFFS = (-205.0 / 72.0, 8.0 / 5.0, -1.0 / 5.0, 8.0 / 315.0, -1.0 / 560.0)
KERNEL = (1.0 / 16.0, 4.0 / 16.0, 6.0 / 16.0, 4.0 / 16.0, 1.0 / 16.0)


def shifted(values, axis, offset):
    size = values.shape[axis]
    width = abs(offset)
    pads = [(0, 0, 0)] * values.ndim
    if offset > 0:
        kept = lax.slice_in_dim(values, offset, size, axis=axis)
        pads[axis] = (0, width, 0)
    else:
        kept = lax.slice_in_dim(values, 0, size - width, axis=axis)
        pads[axis] = (width, 0, 0)
    return lax.pad(kept, jnp.array(0.0, values.dtype), pads)


def band(size):
    index = jnp.arange(size)
    gap = jnp.abs(index[:, None] - index[None, :])
    matrix = jnp.zeros((size, size), jnp.float32)
    for k in range(1, 5):
        matrix = jnp.where(gap == k, jnp.float32(COEFFS[k]), matrix)
    return matrix


def lateral_laplace(core, zaxis):
    rows, cols = core.shape[zaxis + 1], core.shape[zaxis + 2]
    high = lax.Precision.HIGHEST
    along_y = jnp.einsum("...xy,yk->...xk", core, band(cols), precision=high)
    along_x = jnp.einsum("...xy,kx->...ky", core, band(rows), precision=high)
    return 3.0 * COEFFS[0] * core + (along_x + along_y)


def depth_laplace(below, core, above, zaxis):
    planes = core.shape[zaxis]
    extended = jnp.concatenate([below, core, above], axis=zaxis)
    total = None
    for k in range(1, 5):
        near = lax.slice_in_dim(extended, HALO + k, HALO + k + planes, axis=zaxis) + lax.slice_in_dim(
            extended, HALO - k, HALO - k + planes, axis=zaxis
        )
        total = COEFFS[k] * near if total is None else total + COEFFS[k] * near
    return total


def smooth_matrix(size):
    index = jnp.arange(size)
    gap = index[:, None] - index[None, :]
    matrix = jnp.zeros((size, size), jnp.float32)
    for k in range(-2, 3):
        matrix = jnp.where(gap == k, jnp.float32(KERNEL[2 + k]), matrix)
    return matrix


def smooth_lateral(values):
    high = lax.Precision.HIGHEST
    rows, cols = values.shape[-2], values.shape[-1]
    along_y = jnp.einsum("...xy,yk->...xk", values, smooth_matrix(cols), precision=high)
    return jnp.einsum("...xy,kx->...ky", along_y, smooth_matrix(rows), precision=high)


def smooth(values, axis):
    total = KERNEL[2] * values
    for k in (1, 2):
        total = total + KERNEL[2 + k] * (shifted(values, axis, k) + shifted(values, axis, -k))
    return total


def exchange(fields, dim):
    devices = lax.axis_size("depth")
    length = fields[0].shape[dim]
    up = [(i, i + 1) for i in range(devices - 1)]
    down = [(i + 1, i) for i in range(devices - 1)]
    below, above = [], []
    for f in fields:
        above.append(lax.ppermute(lax.slice_in_dim(f, 0, HALO, axis=dim), "depth", down))
        below.append(lax.ppermute(lax.slice_in_dim(f, length - HALO, length, axis=dim), "depth", up))
    return below, above


def spread(flat, values, first_plane, planes, rows, cols):
    lateral = rows * cols
    limit = planes * lateral
    local = flat - first_plane * lateral
    local = jnp.where((local >= 0) & (local < limit), local, limit)
    grid = jnp.zeros((values.shape[0], limit), jnp.float32).at[:, local].add(values, mode="drop")
    return grid.reshape(values.shape[0], planes, rows, cols)


def spread_dense(depth, cell, values, first_plane, planes, rows, cols):
    steps, count = values.shape
    local = depth - first_plane
    inside = (local >= 0) & (local < planes)
    row_id = jnp.where(inside, local * rows + cell // cols, -1)
    by_row = (row_id[None, :] == jnp.arange(planes * rows)[:, None]).astype(jnp.bfloat16)
    by_col = (cell % cols)[:, None] == jnp.arange(cols)[None, :]
    pieces = []
    rest = values
    for _ in range(3):
        piece = lax.reduce_precision(rest, exponent_bits=8, mantissa_bits=7)
        rest = rest - piece
        pieces.append(piece.astype(jnp.bfloat16))
    stacked = jnp.stack(pieces)
    right = jnp.where(by_col[None, None], stacked[:, :, :, None], jnp.zeros((), jnp.bfloat16))
    right = right.transpose(2, 0, 1, 3).reshape(count, 3 * steps * cols)
    grid = jnp.dot(by_row, right, preferred_element_type=jnp.float32)
    grid = grid.reshape(planes * rows, 3, steps, cols)
    grid = grid[:, 0] + grid[:, 1] + grid[:, 2]
    return grid.transpose(1, 0, 2).reshape(steps, planes, rows, cols)


def reduce_shots(values, dim):
    devices = lax.axis_size("shots")
    me = lax.axis_index("shots")
    length = values.shape[dim]
    shape = values.shape
    blocks = values.reshape(shape[:dim] + (devices, length // devices) + shape[dim + 1 :])
    bit = 1
    while bit < devices:
        count = blocks.shape[dim]
        paired = blocks.reshape(shape[:dim] + (count // 2, 2, length // devices) + shape[dim + 1 :])
        mine = (me // bit) % 2
        keep = lax.dynamic_index_in_dim(paired, mine, axis=dim + 1, keepdims=False)
        send = lax.dynamic_index_in_dim(paired, 1 - mine, axis=dim + 1, keepdims=False)
        pairs = [(i, i ^ bit) for i in range(devices)]
        blocks = keep + lax.ppermute(send, "shots", pairs)
        bit *= 2
    return blocks.reshape(shape[:dim] + (length // devices,) + shape[dim + 1 :])


def on_device(
    forward_prev,
    forward_now,
    adjoint_prev,
    adjoint_now,
    courant,
    wavelet,
    sign_bits,
    source_depth,
    source_cell,
    receiver_depth,
    receiver_cell,
    residual_traces,
):
    planes, rows, cols = courant.shape
    lateral = rows * cols
    source_flat = source_depth * lateral + source_cell
    receiver_flat = receiver_depth * lateral + receiver_cell
    signs = (2 * sign_bits - 1).astype(jnp.float32)
    position = lax.axis_index("depth")
    earlier = [forward_prev, adjoint_prev]
    current = [forward_now, adjoint_now]
    zaxis = 1
    below, above = exchange(current, zaxis)
    first_plane = position * planes
    correlation = None
    forward_terms = spread_dense(source_depth, source_cell, signs[0][None, :] * wavelet, first_plane, planes, rows, cols)
    adjoint_terms = spread_dense(receiver_depth, receiver_cell, residual_traces[0], first_plane, planes, rows, cols)
    for step in range(STEPS):
        terms = [forward_terms[step : step + 1], adjoint_terms[step : step + 1]]
        partial = lax.optimization_barrier(
            [
                2.0 * current[i] - earlier[i] + courant * lateral_laplace(current[i], zaxis) + terms[i]
                for i in range(2)
            ]
        )
        fresh = []
        halos = ([], [])
        for i in range(2):
            if i > 0 and step + 1 < STEPS:
                _, below[i], above[i] = lax.optimization_barrier((marker, below[i], above[i]))
            fresh.append(partial[i] + courant * depth_laplace(below[i], current[i], above[i], zaxis))
            if step + 1 < STEPS:
                if i == 0:
                    devices = lax.axis_size("depth")
                    length = fresh[i].shape[zaxis]
                    marker = lax.ppermute(
                        lax.slice_in_dim(fresh[i], length - 1, length, axis=zaxis),
                        "depth",
                        [(j, j + 1) for j in range(devices - 1)],
                    )
                    rest = lax.ppermute(
                        lax.slice_in_dim(fresh[i], length - HALO, length - 1, axis=zaxis),
                        "depth",
                        [(j, j + 1) for j in range(devices - 1)],
                    )
                    leading = lax.ppermute(
                        lax.slice_in_dim(fresh[i], 0, HALO, axis=zaxis),
                        "depth",
                        [(j + 1, j) for j in range(devices - 1)],
                    )
                    halos[0].append(jnp.concatenate([rest, marker], axis=zaxis))
                    halos[1].append(leading)
                else:
                    sent = exchange([fresh[i]], zaxis)
                    halos[0].append(sent[0][0])
                    halos[1].append(sent[1][0])
        if step + 1 < STEPS:
            below, above = halos
        part = fresh[0][0] * fresh[1][0]
        correlation = part if correlation is None else correlation + part
        earlier, current = (current, fresh)
    lateral_smooth = smooth_lateral(correlation)
    reduced = reduce_shots(lateral_smooth, 1)
    columns = lax.all_to_all(reduced, "depth", split_axis=1, concat_axis=0, tiled=True)
    gradient = smooth(columns, 0)
    return (earlier[0], current[0], earlier[1], current[1], gradient)


def solution(mesh):
    in_specs = (
        P("shots", "depth", None, None),
        P("shots", "depth", None, None),
        P("shots", "depth", None, None),
        P("shots", "depth", None, None),
        P("depth", None, None),
        P(),
        P("shots", None),
        P(),
        P(),
        P(),
        P(),
        P("shots", None, None),
    )
    out_specs = (
        P("shots", "depth", None, None),
        P("shots", "depth", None, None),
        P("shots", "depth", None, None),
        P("shots", "depth", None, None),
        P(None, ("shots", "depth"), None),
    )
    return jax.shard_map(
        on_device, mesh=mesh, in_specs=in_specs, out_specs=out_specs, check_vma=False
    )
```
